512 devices in a mesh: tm: 32 (over z, core), band: 4 (over y), fsdp: 4 (over x).
Axes of the slice: x: 4, y: 4, z: 16, core: 2. Of those that a mesh axis runs over, the one named last changes fastest.
Arguments:
- video: bfloat16 [128, 64, 128, 256], P('tm', 'band', 'fsdp'), may hold values from -8 to 8
- clip_lengths: int32 [16], replicated, may hold values from 1 to 31, 128 in all
- norm_gains: float32 [2, 256], replicated, may hold values from 0.1 to 1.9
- spatial_kernel_weight: bfloat16 [256, 2304], P(('band', 'fsdp')), may hold values from -0.125 to 0.125
- w_time: bfloat16 [256, 768], P(('band', 'fsdp')), may hold values from -0.21875 to 0.21875
- w_qkv: bfloat16 [256, 768], P(('band', 'fsdp')), may hold values from -4 to 4
- w_out: bfloat16 [256, 256], P(('band', 'fsdp')), may hold values from -0.375 to 0.375
Outputs:
- mixed: bfloat16 [4, 4, 512, 128, 256], P('band', 'fsdp', 'tm')
The draws below stay inside these ranges and needn't reach their ends.
Inputs may be any that keep to these rules, and one draw needn't show every extreme that they name: `clip_lengths`: every clip has at least one frame and the lengths sum to 128.
All inputs are finite; a program needn't handle non-finite values.
Results may differ from the reference program's by a relative error of at most 0.0064.
Values may be sent and summed in bfloat16 or wider, within the bound.
No kernel may reach another device: no remote copies, remote signals or barrier semaphores. Data moves between devices by JAX's collectives and lax.ppermute only.
A program may use at most 64 MiB of HBM per device.

```python
import math
import jax
import jax.numpy as jnp
import numpy as np
from jax import lax

C = 256
GROUPS = 32
ROWS_DEV = 16
COLUMNS_PER_SHARD = 32
FRAMES = 128
H = 64
W = 128
NCLIPS = 16
MOSTLEN = 31
BANDS = 4
COLBLK = 4


def draw_video(key, part):
    key_base = jax.random.fold_in(key, 11)
    key_rough = jax.random.fold_in(key, 12)
    key_level = jax.random.fold_in(key, 13)
    key_offset = jax.random.fold_in(key, 14)
    cell_rows = ROWS_DEV // 2
    cell_cols = COLUMNS_PER_SHARD // 2
    grid_rows = H // cell_rows
    grid_cols = W // cell_cols
    level = jnp.exp(jax.random.uniform(key_level, (FRAMES, grid_rows, grid_cols, 1), jnp.float32, -1.15, 1.15))
    level = jnp.repeat(jnp.repeat(level, cell_rows, axis=1), cell_cols, axis=2)
    offset = jax.random.uniform(key_offset, (FRAMES, grid_rows, grid_cols, GROUPS), jnp.float32, -0.6, 0.6)
    offset = jnp.repeat(jnp.repeat(jnp.repeat(offset, cell_rows, axis=1), cell_cols, axis=2), C // GROUPS, axis=3)
    rough = jax.random.uniform(key_rough, (FRAMES, H, W, 1), jnp.float32, 0.7, 1.3)
    base = jax.random.normal(key_base, (FRAMES, H, W, C), jnp.float32)
    whole = (0.8 * base * rough + offset) * level
    return jnp.clip(whole, -8.0, 8.0).astype(jnp.bfloat16)


def draw_w_qkv(key, part):
    scale = 1.0 / jnp.sqrt(jnp.float32(C))
    keys_part = jax.random.normal(jax.random.fold_in(key, 21), (C, C), jnp.float32) * scale
    values_part = jax.random.normal(jax.random.fold_in(key, 22), (C, C), jnp.float32) * scale
    noise = jax.random.normal(jax.random.fold_in(key, 23), (C, C), jnp.float32) * scale
    query_part = noise
    whole = jnp.concatenate([query_part, keys_part, values_part], axis=1)
    return jnp.clip(whole, -4.0, 4.0).astype(jnp.bfloat16)


def levels(rng, dims, split, smallest, high):
    def one(dim, shards_of):
        steps = jax.random.uniform(jax.random.fold_in(jax.random.fold_in(rng, 6), dim), (shards_of,), jnp.float32, smallest / len(split), high / len(split))
        return jnp.repeat(jnp.exp(steps), dims[dim] // shards_of).reshape((-1,) + (1,) * (len(dims) - dim - 1))

    level = one(*split[0])
    for cut in split[1:]:
        level = level * one(*cut)
    return level


def length_profile(amount, total, limit, skew):
    loads = [(1 << 20) // math.isqrt(rank ** skew) + 1 for rank in range(2, amount + 1)]
    surplus, counts = total - limit - (amount - 1), [1] * (amount - 1)
    while surplus > 0:
        candidates = [i for i in range(amount - 1) if counts[i] < limit]
        whole, remaining = sum([loads[i] for i in candidates]), surplus
        for i in candidates:
            extra = min(limit - counts[i], max(1, remaining * loads[i] // whole), surplus)
            counts[i] = counts[i] + extra
            surplus = surplus - extra
    return np.array([limit] + counts)


def uneven_parts(key, number_of, total, most, skew):
    if number_of == 2:
        one = jax.random.randint(key, (), max(1, total - most), min(most, total - 1) + 1)
        return jnp.stack([one, total - one])
    lengths = jnp.asarray(length_profile(number_of, total, most, skew), jnp.int32)
    couples = (number_of - 1) // 2
    donor, receiver = lengths[1:1 + 2 * couples:2], lengths[2:2 + 2 * couples:2]
    slack = jnp.minimum(donor - 1, most - receiver)
    passed = jax.random.randint(jax.random.fold_in(key, 1), (couples,), 0, 1 << 20) % (slack + 1)
    lengths = lengths.at[1:1 + 2 * couples:2].set(donor - passed).at[2:2 + 2 * couples:2].set(receiver + passed)
    return lengths[jax.random.permutation(jax.random.fold_in(key, 2), number_of)]


def centred(rng, shape, spread, most, cuts=(), held_as=jnp.bfloat16):
    array = jax.random.normal(rng, shape, jnp.float32) * spread
    if len(cuts) > 0:
        array = levels(rng, shape, cuts, -0.22, 0.18) * array
    return jnp.clip(array, min=-most, max=most).astype(held_as)


def setup_inputs(seed: int = 0) -> dict:
    key_list = jax.random.split(jax.random.key(seed), 8)
    video = draw_video(jax.random.fold_in(key_list[7], 71), 0)
    clip_lengths = uneven_parts(key_list[1], NCLIPS, FRAMES, MOSTLEN, 1).astype(jnp.int32)
    norm_gains = jnp.clip(1.0 + 0.18 * jax.random.normal(key_list[2], (2, C), jnp.float32), 0.1, 1.9)
    spatial_kernel_weight = centred(key_list[3], (C, 9 * C), (9 * C) ** -0.5, 0.125, ((0, 16),))
    w_time = centred(key_list[4], (C, 3 * C), (3 * C) ** -0.5, 0.21875, ((0, 16),))
    w_qkv = draw_w_qkv(jax.random.fold_in(key_list[7], 71), 0)
    w_out = centred(key_list[6], (C, C), C ** -0.5, 0.375, ((0, 16),))
    return {"video": video, "clip_lengths": clip_lengths, "norm_gains": norm_gains, "spatial_kernel_weight": spatial_kernel_weight, "w_time": w_time, "w_qkv": w_qkv, "w_out": w_out}


EPS = 1e-06

def frame_starts(clip_lengths, total):
    ends = jnp.cumsum(clip_lengths).astype(jnp.int32)
    begins = (ends - clip_lengths).astype(jnp.int32)
    index = jnp.arange(total, dtype=jnp.int32)
    chosen = jnp.where(begins[None, :] <= index[:, None], begins[None, :], 0)
    return lax.optimization_barrier(jnp.max(chosen, axis=1)).astype(jnp.int32)

def norm_frame(field, gain):
    height, width, chans = field.shape
    group_width = chans // GROUPS
    vals = field.astype(jnp.float32).reshape(height * width, GROUPS, group_width)
    count = height * width * group_width
    mean = lax.optimization_barrier(jnp.sum(vals, axis=(0, 2))) / count
    square = lax.optimization_barrier(jnp.sum(vals * vals, axis=(0, 2))) / count
    scale = lax.rsqrt(square - mean * mean + EPS)
    normed = (vals - mean[None, :, None]) * scale[None, :, None]
    return normed.reshape(height, width, chans) * gain

def space_conv(act, spatial_kernel_weight):
    height, width, chans = act.shape
    padded = jnp.pad(act, ((1, 1), (1, 1), (0, 0)))
    total = jnp.zeros((height, width, chans), jnp.float32)
    for tap in range(9):
        shift_y = tap // 3
        shift_x = tap % 3
        total = total + jnp.dot(padded[shift_y:shift_y + height, shift_x:shift_x + width], spatial_kernel_weight[:, tap * chans:(tap + 1) * chans], preferred_element_type=jnp.float32)
    return total

def reference(video, clip_lengths, norm_gains, spatial_kernel_weight, w_time, w_qkv, w_out):
    starts = frame_starts(clip_lengths, FRAMES)

    def first_section(frame):
        act = jax.nn.silu(norm_frame(frame, norm_gains[0])).astype(jnp.bfloat16)
        return space_conv(act, spatial_kernel_weight).astype(jnp.bfloat16)
    spatial = lax.map(first_section, video)

    def time_frame(index):
        total = lax.dynamic_index_in_dim(video, index, 0, keepdims=False).astype(jnp.float32)
        for tap in range(3):
            source = jnp.maximum(index - 2 + tap, starts[index]).astype(jnp.int32)
            piece = lax.dynamic_index_in_dim(spatial, source, 0, keepdims=False)
            total = total + jnp.dot(piece, w_time[:, tap * C:(tap + 1) * C], preferred_element_type=jnp.float32)
        return total.astype(jnp.bfloat16)
    resid = lax.map(time_frame, jnp.arange(FRAMES, dtype=jnp.int32))
    normed = lax.map(lambda frame: norm_frame(frame, norm_gains[1]).astype(jnp.bfloat16), resid)
    index = jnp.arange(FRAMES, dtype=jnp.int32)
    allowed = (index[None, :] <= index[:, None]) & (index[None, :] >= starts[:, None])

    def attend_query_row(row):
        rows_in = lax.dynamic_index_in_dim(normed, row, 1, keepdims=False)
        resid_row = lax.dynamic_index_in_dim(resid, row, 1, keepdims=False)
        qkv = jnp.dot(rows_in, w_qkv, preferred_element_type=jnp.float32).astype(jnp.bfloat16)
        query = qkv[..., :C].astype(jnp.float32)
        keys = qkv[..., C:2 * C].astype(jnp.float32)
        value_rows = qkv[..., 2 * C:].astype(jnp.float32)
        scores = jnp.einsum('fwc,gwc->wfg', query, keys) / math.sqrt(C)
        scores = jnp.where(allowed[None], scores, -1e+30)
        top = lax.optimization_barrier(jnp.max(scores, axis=-1, keepdims=True))
        expo = jnp.where(allowed[None], jnp.exp(scores - top), 0.0)
        attention_probabilities = (expo / lax.optimization_barrier(jnp.sum(expo, axis=-1, keepdims=True))).astype(jnp.bfloat16)
        attention_output = jnp.einsum('wfg,gwc->wfc', attention_probabilities.astype(jnp.float32), value_rows).astype(jnp.bfloat16)
        projected_output = jnp.dot(attention_output, w_out, preferred_element_type=jnp.float32)
        return (jnp.swapaxes(resid_row, 0, 1).astype(jnp.float32) + projected_output).astype(jnp.bfloat16)
    rows_out = lax.map(attend_query_row, jnp.arange(H, dtype=jnp.int32))
    blocks = rows_out.reshape(BANDS, ROWS_DEV, COLBLK, COLUMNS_PER_SHARD, FRAMES, C)
    blocks = jnp.transpose(blocks, (0, 2, 1, 3, 4, 5))
    return blocks.reshape(BANDS, COLBLK, ROWS_DEV * COLUMNS_PER_SHARD, FRAMES, C)
```

```python
import math

import jax
import jax.numpy as jnp
from jax import lax
from jax.sharding import PartitionSpec as P

GROUPS = 32


EPS = 1e-06


def with_halo(x, sides, width):
    for axis, dim in sides:
        size, length = (lax.axis_size(axis), x.shape[dim])
        up = [(i, (i + 1) % size) for i in range(size - 1)]
        down = [(j, i) for i, j in up]
        last = lax.slice_in_dim(x, length - width, length, axis=dim)
        initial = lax.slice_in_dim(x, 0, width, axis=dim)
        before = lax.ppermute(last, axis, up)
        after = lax.ppermute(initial, axis, down)
        x = jnp.concatenate([before, x, after], axis=dim)
    return x


def from_behind(x, axis, by):
    length = lax.axis_size(axis)
    pairs = [(i, i + by) for i in range(length) if 0 <= i + by < length]
    return lax.ppermute(x, axis, pairs)


def butterfly_sum(x, axes):
    for axis in axes:
        size = lax.axis_size(axis)
        step = 1
        while step < size:
            pairs = [(i, i ^ step) for i in range(size)]
            x = x + lax.ppermute(x, axis, pairs)
            step *= 2
    return x


def frame_starts(clip_lengths, total):
    ends = jnp.cumsum(clip_lengths)
    begins = ends - clip_lengths
    index = jnp.arange(total, dtype=jnp.int32)
    chosen = jnp.where(begins[None, :] <= index[:, None], begins[None, :], 0)
    return jnp.max(chosen, axis=1)


def group_moments(field):
    frames, height, width, chans = field.shape
    group_width = chans // GROUPS
    vals = field.astype(jnp.float32).reshape(frames, height * width, GROUPS, group_width)
    sums = jnp.sum(vals, axis=(1, 3))
    squares = jnp.sum(vals * vals, axis=(1, 3))
    both = butterfly_sum(jnp.stack([sums, squares]), ("band", "fsdp"))
    sums, squares = both[0], both[1]
    count = height * width * group_width * lax.axis_size("band") * lax.axis_size("fsdp")
    mean = sums / count
    scale = lax.rsqrt(squares / count - mean * mean + EPS)
    return (mean, scale)


def apply_norm(field, mean, scale, gain):
    shape = field.shape
    chans = shape[-1]
    group_width = chans // GROUPS
    vals = field.astype(jnp.float32).reshape(shape[0], -1, GROUPS, group_width)
    normed = (vals - mean[:, None, :, None]) * scale[:, None, :, None]
    return normed.reshape(shape) * gain


def split3(x):
    hi = lax.reduce_precision(x, exponent_bits=8, mantissa_bits=7)
    rest = x - hi
    mid = lax.reduce_precision(rest, exponent_bits=8, mantissa_bits=7)
    lo = rest - mid
    return jnp.stack([hi, mid, lo]).astype(jnp.bfloat16)


def join3(pieces):
    pieces = pieces.astype(jnp.float32)
    return (pieces[0] + pieces[1]) + pieces[2]


def body(video, clip_lengths, norm_gains, spatial_kernel_weight, w_time, w_qkv, w_out):
    frames, height, width, chans = video.shape
    widths = [w.shape[1] for w in (spatial_kernel_weight, w_time, w_qkv, w_out)]
    packed = jnp.concatenate([spatial_kernel_weight, w_time, w_qkv, w_out], axis=1)
    gathered = lax.all_gather(packed, ("band", "fsdp"), axis=0, tiled=True)
    offsets = [sum(widths[:i]) for i in range(4)]
    space_full, time_full, qkv_full, output_complete = [
        gathered[:, o : o + w] for o, w in zip(offsets, widths)
    ]
    ranks = lax.axis_size("tm")
    total_frames = frames * ranks
    first = lax.axis_index("tm") * frames
    starts = frame_starts(clip_lengths, total_frames)
    local_starts = lax.dynamic_slice_in_dim(starts, first, frames)
    mean_one, scale_one = group_moments(video)
    act = jax.nn.silu(apply_norm(video, mean_one, scale_one, norm_gains[0])).astype(jnp.bfloat16)
    padded = with_halo(act, (("band", 1), ("fsdp", 2)), 1)
    spatial = jnp.zeros((frames, height, width, chans), jnp.float32)
    for tap in range(9):
        shift_y = tap // 3
        shift_x = tap % 3
        spatial = spatial + jnp.einsum(
            "fhwc,cd->fhwd",
            padded[:, shift_y : shift_y + height, shift_x : shift_x + width],
            space_full[:, tap * chans : (tap + 1) * chans],
            preferred_element_type=jnp.float32,
        )
    spatial = spatial.astype(jnp.bfloat16)
    carried = from_behind(spatial[frames - 2 :], "tm", 1)
    extended = jnp.concatenate([carried, spatial], axis=0)
    position = first + jnp.arange(frames, dtype=jnp.int32)
    slots = jnp.arange(frames + 2, dtype=jnp.int32)
    temporal = jnp.zeros((frames, height, width, chans), jnp.float32)
    for tap in range(3):
        source = jnp.maximum(position - 2 + tap, local_starts) - first + 2
        select = (source[:, None] == slots[None, :]).astype(jnp.bfloat16)
        picked = jnp.einsum(
            "fe,ehwc->fhwc", select, extended, preferred_element_type=jnp.float32
        ).astype(jnp.bfloat16)
        temporal = temporal + jnp.einsum(
            "fhwc,cd->fhwd",
            picked,
            time_full[:, tap * chans : (tap + 1) * chans],
            preferred_element_type=jnp.float32,
        )
    resid = (video.astype(jnp.float32) + temporal).astype(jnp.bfloat16)
    mean_two, scale_two = group_moments(resid)
    pixels = height * width
    group_pixels = pixels // ranks
    flat_resid = resid.reshape(frames, ranks, group_pixels, chans).transpose(1, 0, 2, 3)
    stats = split3(jnp.concatenate([mean_two, scale_two], axis=1))
    stats = stats.transpose(1, 0, 2).reshape(frames, 3 * 2 * GROUPS)
    stats = jnp.pad(stats, ((0, 0), (0, chans - stats.shape[1])))
    stats_rows = jnp.broadcast_to(stats[None, :, None, :], (ranks, frames, 1, chans))
    payload = jnp.concatenate([flat_resid, stats_rows], axis=2)
    received = lax.all_to_all(payload, "tm", split_axis=0, concat_axis=0, tiled=True)
    resid_time = received[:, :, :group_pixels, :].reshape(total_frames, group_pixels, chans)
    got = received[:, :, group_pixels, : 3 * 2 * GROUPS].reshape(total_frames, 3, 2 * GROUPS)
    moments = join3(got.transpose(1, 0, 2))
    mean_all, scale_all = moments[:, :GROUPS], moments[:, GROUPS:]
    flat_norm = apply_norm(resid_time, mean_all, scale_all, norm_gains[1]).astype(jnp.bfloat16)
    qkv_time = jnp.einsum(
        "fpc,cd->fpd", flat_norm, qkv_full, preferred_element_type=jnp.float32
    ).astype(jnp.bfloat16)
    query = qkv_time[..., :chans]
    keys = qkv_time[..., chans : 2 * chans]
    value_rows = qkv_time[..., 2 * chans :]
    index = jnp.arange(total_frames, dtype=jnp.int32)
    allowed = (index[None, :] <= index[:, None]) & (index[None, :] >= starts[:, None])
    scores = jnp.einsum(
        "fpc,gpc->pfg", query, keys, preferred_element_type=jnp.float32
    ) / math.sqrt(chans)
    scores = jnp.where(allowed[None], scores, -1e30)
    top = jnp.max(scores, axis=-1, keepdims=True)
    expo = jnp.where(allowed[None], jnp.exp(scores - top), 0.0)
    attention_probabilities = (expo / jnp.sum(expo, axis=-1, keepdims=True)).astype(jnp.bfloat16)
    attention_output = jnp.einsum(
        "boh,hba->boa", attention_probabilities, value_rows, preferred_element_type=jnp.float32
    ).astype(jnp.bfloat16)
    projected_output = jnp.einsum(
        "axi,iy->axy", attention_output, output_complete, preferred_element_type=jnp.float32
    )
    mixed = (jnp.swapaxes(resid_time, 0, 1).astype(jnp.float32) + projected_output).astype(
        jnp.bfloat16
    )
    return mixed.reshape(1, 1, mixed.shape[0], total_frames, chans)


def solution(mesh):
    return jax.shard_map(
        body,
        mesh=mesh,
        in_specs=(
            P("tm", "band", "fsdp", None),
            P(),
            P(),
            P(("band", "fsdp"), None),
            P(("band", "fsdp"), None),
            P(("band", "fsdp"), None),
            P(("band", "fsdp"), None),
        ),
        out_specs=P("band", "fsdp", "tm", None, None),
        check_vma=False,
    )
```

```python
import math

import jax
import jax.numpy as jnp
from jax import lax
from jax.sharding import PartitionSpec as P

GROUPS = 32


EPS = 1e-06


def with_halo(x, sides, width):
    for axis, dim in sides:
        size, length = (lax.axis_size(axis), x.shape[dim])
        up = [(i, (i + 1) % size) for i in range(size - 1)]
        down = [(j, i) for i, j in up]
        last = lax.slice_in_dim(x, length - width, length, axis=dim)
        initial = lax.slice_in_dim(x, 0, width, axis=dim)
        before = lax.ppermute(last, axis, up)
        after = lax.ppermute(initial, axis, down)
        x = jnp.concatenate([before, x, after], axis=dim)
    return x


def from_behind(x, axis, by):
    length = lax.axis_size(axis)
    pairs = [(i, i + by) for i in range(length) if 0 <= i + by < length]
    return lax.ppermute(x, axis, pairs)


def butterfly_sum(x, axes):
    for axis in axes:
        size = lax.axis_size(axis)
        step = 1
        while step < size:
            pairs = [(i, i ^ step) for i in range(size)]
            x = x + lax.ppermute(x, axis, pairs)
            step *= 2
    return x


def frame_starts(clip_lengths, total):
    ends = jnp.cumsum(clip_lengths)
    begins = ends - clip_lengths
    index = jnp.arange(total, dtype=jnp.int32)
    chosen = jnp.where(begins[None, :] <= index[:, None], begins[None, :], 0)
    return jnp.max(chosen, axis=1)


def group_moments(field):
    frames, height, width, chans = field.shape
    group_width = chans // GROUPS
    vals = field.astype(jnp.float32).reshape(frames, height * width, GROUPS, group_width)
    sums = jnp.sum(vals, axis=(1, 3))
    squares = jnp.sum(vals * vals, axis=(1, 3))
    both = butterfly_sum(jnp.stack([sums, squares]), ("band", "fsdp"))
    sums, squares = both[0], both[1]
    count = height * width * group_width * lax.axis_size("band") * lax.axis_size("fsdp")
    mean = sums / count
    scale = lax.rsqrt(squares / count - mean * mean + EPS)
    return (mean, scale)


def apply_norm(field, mean, scale, gain):
    shape = field.shape
    chans = shape[-1]
    group_width = chans // GROUPS
    vals = field.astype(jnp.float32).reshape(shape[0], -1, GROUPS, group_width)
    normed = (vals - mean[:, None, :, None]) * scale[:, None, :, None]
    return normed.reshape(shape) * gain


def body(video, clip_lengths, norm_gains, spatial_kernel_weight, w_time, w_qkv, w_out):
    frames, height, width, chans = video.shape
    widths = [w.shape[1] for w in (spatial_kernel_weight, w_time, w_qkv, w_out)]
    packed = jnp.concatenate([spatial_kernel_weight, w_time, w_qkv, w_out], axis=1)
    gathered = lax.all_gather(packed, ("band", "fsdp"), axis=0, tiled=True)
    offsets = [sum(widths[:i]) for i in range(4)]
    space_full, time_full, qkv_full, output_complete = [
        gathered[:, o : o + w] for o, w in zip(offsets, widths)
    ]
    ranks = lax.axis_size("tm")
    total_frames = frames * ranks
    first = lax.axis_index("tm") * frames
    starts = frame_starts(clip_lengths, total_frames)
    local_starts = lax.dynamic_slice_in_dim(starts, first, frames)
    mean_one, scale_one = group_moments(video)
    act = jax.nn.silu(apply_norm(video, mean_one, scale_one, norm_gains[0])).astype(jnp.bfloat16)
    padded = with_halo(act, (("band", 1), ("fsdp", 2)), 1)
    spatial = jnp.zeros((frames, height, width, chans), jnp.float32)
    for tap in range(9):
        shift_y = tap // 3
        shift_x = tap % 3
        spatial = spatial + jnp.einsum(
            "fhwc,cd->fhwd",
            padded[:, shift_y : shift_y + height, shift_x : shift_x + width],
            space_full[:, tap * chans : (tap + 1) * chans],
            preferred_element_type=jnp.float32,
        )
    spatial = spatial.astype(jnp.bfloat16)
    carried = from_behind(spatial[frames - 2 :], "tm", 1)
    extended = jnp.concatenate([carried, spatial], axis=0)
    position = first + jnp.arange(frames, dtype=jnp.int32)
    slots = jnp.arange(frames + 2, dtype=jnp.int32)
    temporal = jnp.zeros((frames, height, width, chans), jnp.float32)
    for tap in range(3):
        source = jnp.maximum(position - 2 + tap, local_starts) - first + 2
        select = (source[:, None] == slots[None, :]).astype(jnp.bfloat16)
        picked = jnp.einsum(
            "fe,ehwc->fhwc", select, extended, preferred_element_type=jnp.float32
        ).astype(jnp.bfloat16)
        temporal = temporal + jnp.einsum(
            "fhwc,cd->fhwd",
            picked,
            time_full[:, tap * chans : (tap + 1) * chans],
            preferred_element_type=jnp.float32,
        )
    resid = (video.astype(jnp.float32) + temporal).astype(jnp.bfloat16)
    pixels = height * width
    group_pixels = pixels // ranks
    flat_resid = resid.reshape(frames, ranks, group_pixels, chans).transpose(1, 0, 2, 3)
    received = lax.all_to_all(flat_resid, "tm", split_axis=0, concat_axis=0, tiled=True)
    resid_time = received.reshape(total_frames, group_pixels, chans)
    mean_two, scale_two = group_moments(resid)
    moments = lax.all_gather(
        jnp.concatenate([mean_two, scale_two], axis=1), "tm", axis=0, tiled=True
    )
    mean_all, scale_all = moments[:, :GROUPS], moments[:, GROUPS:]
    flat_norm = apply_norm(resid_time, mean_all, scale_all, norm_gains[1]).astype(jnp.bfloat16)
    qkv_time = jnp.einsum(
        "fpc,cd->fpd", flat_norm, qkv_full, preferred_element_type=jnp.float32
    ).astype(jnp.bfloat16)
    query = qkv_time[..., :chans]
    keys = qkv_time[..., chans : 2 * chans]
    value_rows = qkv_time[..., 2 * chans :]
    index = jnp.arange(total_frames, dtype=jnp.int32)
    allowed = (index[None, :] <= index[:, None]) & (index[None, :] >= starts[:, None])
    scores = jnp.einsum(
        "fpc,gpc->pfg", query, keys, preferred_element_type=jnp.float32
    ) / math.sqrt(chans)
    scores = jnp.where(allowed[None], scores, -1e30)
    top = jnp.max(scores, axis=-1, keepdims=True)
    expo = jnp.where(allowed[None], jnp.exp(scores - top), 0.0)
    attention_probabilities = (expo / jnp.sum(expo, axis=-1, keepdims=True)).astype(jnp.bfloat16)
    attention_output = jnp.einsum(
        "boh,hba->boa", attention_probabilities, value_rows, preferred_element_type=jnp.float32
    ).astype(jnp.bfloat16)
    projected_output = jnp.einsum(
        "axi,iy->axy", attention_output, output_complete, preferred_element_type=jnp.float32
    )
    mixed = (jnp.swapaxes(resid_time, 0, 1).astype(jnp.float32) + projected_output).astype(
        jnp.bfloat16
    )
    return mixed.reshape(1, 1, mixed.shape[0], total_frames, chans)


def solution(mesh):
    return jax.shard_map(
        body,
        mesh=mesh,
        in_specs=(
            P("tm", "band", "fsdp", None),
            P(),
            P(),
            P(("band", "fsdp"), None),
            P(("band", "fsdp"), None),
            P(("band", "fsdp"), None),
            P(("band", "fsdp"), None),
        ),
        out_specs=P("band", "fsdp", "tm", None, None),
        check_vma=False,
    )
```

```python
import math

import jax
import jax.numpy as jnp
from jax import lax
from jax.sharding import PartitionSpec as P

GROUPS = 32


EPS = 1e-06


def with_halo(x, sides, width):
    for axis, dim in sides:
        size, length = (lax.axis_size(axis), x.shape[dim])
        up = [(i, (i + 1) % size) for i in range(size - 1)]
        down = [(j, i) for i, j in up]
        last = lax.slice_in_dim(x, length - width, length, axis=dim)
        initial = lax.slice_in_dim(x, 0, width, axis=dim)
        before = lax.ppermute(last, axis, up)
        after = lax.ppermute(initial, axis, down)
        x = jnp.concatenate([before, x, after], axis=dim)
    return x


def from_behind(x, axis, by):
    length = lax.axis_size(axis)
    pairs = [(i, i + by) for i in range(length) if 0 <= i + by < length]
    return lax.ppermute(x, axis, pairs)


def butterfly_sum(x, axes):
    for axis in axes:
        size = lax.axis_size(axis)
        step = 1
        while step < size:
            pairs = [(i, i ^ step) for i in range(size)]
            x = x + lax.ppermute(x, axis, pairs)
            step *= 2
    return x


def frame_starts(clip_lengths, total):
    ends = jnp.cumsum(clip_lengths)
    begins = ends - clip_lengths
    index = jnp.arange(total, dtype=jnp.int32)
    chosen = jnp.where(begins[None, :] <= index[:, None], begins[None, :], 0)
    return jnp.max(chosen, axis=1)


def group_moments(field):
    frames, height, width, chans = field.shape
    group_width = chans // GROUPS
    vals = field.astype(jnp.float32).reshape(frames, height * width, GROUPS, group_width)
    sums = jnp.sum(vals, axis=(1, 3))
    squares = jnp.sum(vals * vals, axis=(1, 3))
    both = butterfly_sum(jnp.stack([sums, squares]), ("band", "fsdp"))
    sums, squares = both[0], both[1]
    count = height * width * group_width * lax.axis_size("band") * lax.axis_size("fsdp")
    mean = sums / count
    scale = lax.rsqrt(squares / count - mean * mean + EPS)
    return (mean, scale)


def apply_norm(field, mean, scale, gain):
    shape = field.shape
    chans = shape[-1]
    group_width = chans // GROUPS
    vals = field.astype(jnp.float32).reshape(shape[0], -1, GROUPS, group_width)
    normed = (vals - mean[:, None, :, None]) * scale[:, None, :, None]
    return normed.reshape(shape) * gain


def body(video, clip_lengths, norm_gains, spatial_kernel_weight, w_time, w_qkv, w_out):
    frames, height, width, chans = video.shape
    widths = [w.shape[1] for w in (spatial_kernel_weight, w_time, w_qkv, w_out)]
    packed = jnp.concatenate([spatial_kernel_weight, w_time, w_qkv, w_out], axis=1)
    gathered = lax.all_gather(packed, ("band", "fsdp"), axis=0, tiled=True)
    offsets = [sum(widths[:i]) for i in range(4)]
    space_full, time_full, qkv_full, output_complete = [
        gathered[:, o : o + w] for o, w in zip(offsets, widths)
    ]
    ranks = lax.axis_size("tm")
    total_frames = frames * ranks
    first = lax.axis_index("tm") * frames
    starts = frame_starts(clip_lengths, total_frames)
    local_starts = lax.dynamic_slice_in_dim(starts, first, frames)
    mean_one, scale_one = group_moments(video)
    act = jax.nn.silu(apply_norm(video, mean_one, scale_one, norm_gains[0])).astype(jnp.bfloat16)
    padded = with_halo(act, (("band", 1), ("fsdp", 2)), 1)
    spatial = jnp.zeros((frames, height, width, chans), jnp.float32)
    for tap in range(9):
        shift_y = tap // 3
        shift_x = tap % 3
        spatial = spatial + jnp.einsum(
            "fhwc,cd->fhwd",
            padded[:, shift_y : shift_y + height, shift_x : shift_x + width],
            space_full[:, tap * chans : (tap + 1) * chans],
            preferred_element_type=jnp.float32,
        )
    spatial = spatial.astype(jnp.bfloat16)
    carried = from_behind(spatial[frames - 2 :], "tm", 1)
    extended = jnp.concatenate([carried, spatial], axis=0)
    position = first + jnp.arange(frames, dtype=jnp.int32)
    slots = jnp.arange(frames + 2, dtype=jnp.int32)
    temporal = jnp.zeros((frames, height, width, chans), jnp.float32)
    for tap in range(3):
        source = jnp.maximum(position - 2 + tap, local_starts) - first + 2
        select = (source[:, None] == slots[None, :]).astype(jnp.bfloat16)
        picked = jnp.einsum(
            "fe,ehwc->fhwc", select, extended, preferred_element_type=jnp.float32
        ).astype(jnp.bfloat16)
        temporal = temporal + jnp.einsum(
            "fhwc,cd->fhwd",
            picked,
            time_full[:, tap * chans : (tap + 1) * chans],
            preferred_element_type=jnp.float32,
        )
    resid = (video.astype(jnp.float32) + temporal).astype(jnp.bfloat16)
    pixels = height * width
    group_pixels = pixels // ranks
    flat_resid = resid.reshape(frames, ranks, group_pixels, chans).transpose(1, 0, 2, 3)
    received = lax.all_to_all(flat_resid, "tm", split_axis=0, concat_axis=0, tiled=True)
    resid_time = received.reshape(total_frames, group_pixels, chans)
    mean_two, scale_two = group_moments(resid)
    mine = jnp.concatenate([mean_two, scale_two], axis=1)
    placed = jnp.zeros((ranks, frames, 2 * GROUPS), jnp.float32)
    placed = lax.dynamic_update_index_in_dim(placed, mine, lax.axis_index("tm"), 0)
    moments = butterfly_sum(placed, ("tm",)).reshape(total_frames, 2 * GROUPS)
    mean_all, scale_all = moments[:, :GROUPS], moments[:, GROUPS:]
    flat_norm = apply_norm(resid_time, mean_all, scale_all, norm_gains[1]).astype(jnp.bfloat16)
    qkv_time = jnp.einsum(
        "fpc,cd->fpd", flat_norm, qkv_full, preferred_element_type=jnp.float32
    ).astype(jnp.bfloat16)
    query = qkv_time[..., :chans]
    keys = qkv_time[..., chans : 2 * chans]
    value_rows = qkv_time[..., 2 * chans :]
    index = jnp.arange(total_frames, dtype=jnp.int32)
    allowed = (index[None, :] <= index[:, None]) & (index[None, :] >= starts[:, None])
    scores = jnp.einsum(
        "fpc,gpc->pfg", query, keys, preferred_element_type=jnp.float32
    ) / math.sqrt(chans)
    scores = jnp.where(allowed[None], scores, -1e30)
    top = jnp.max(scores, axis=-1, keepdims=True)
    expo = jnp.where(allowed[None], jnp.exp(scores - top), 0.0)
    attention_probabilities = (expo / jnp.sum(expo, axis=-1, keepdims=True)).astype(jnp.bfloat16)
    attention_output = jnp.einsum(
        "boh,hba->boa", attention_probabilities, value_rows, preferred_element_type=jnp.float32
    ).astype(jnp.bfloat16)
    projected_output = jnp.einsum(
        "axi,iy->axy", attention_output, output_complete, preferred_element_type=jnp.float32
    )
    mixed = (jnp.swapaxes(resid_time, 0, 1).astype(jnp.float32) + projected_output).astype(
        jnp.bfloat16
    )
    return mixed.reshape(1, 1, mixed.shape[0], total_frames, chans)


def solution(mesh):
    return jax.shard_map(
        body,
        mesh=mesh,
        in_specs=(
            P("tm", "band", "fsdp", None),
            P(),
            P(),
            P(("band", "fsdp"), None),
            P(("band", "fsdp"), None),
            P(("band", "fsdp"), None),
            P(("band", "fsdp"), None),
        ),
        out_specs=P("band", "fsdp", "tm", None, None),
        check_vma=False,
    )
```

```python
import math

import jax
import jax.numpy as jnp
from jax import lax
from jax.sharding import PartitionSpec as P

GROUPS = 32


EPS = 1e-06


def with_halo(x, sides, width):
    for axis, dim in sides:
        size, length = (lax.axis_size(axis), x.shape[dim])
        up = [(i, (i + 1) % size) for i in range(size - 1)]
        down = [(j, i) for i, j in up]
        last = lax.slice_in_dim(x, length - width, length, axis=dim)
        initial = lax.slice_in_dim(x, 0, width, axis=dim)
        before = lax.ppermute(last, axis, up)
        after = lax.ppermute(initial, axis, down)
        x = jnp.concatenate([before, x, after], axis=dim)
    return x


def from_behind(x, axis, by):
    length = lax.axis_size(axis)
    pairs = [(i, i + by) for i in range(length) if 0 <= i + by < length]
    return lax.ppermute(x, axis, pairs)


def butterfly_sum(x, axes):
    for axis in axes:
        size = lax.axis_size(axis)
        step = 1
        while step < size:
            pairs = [(i, i ^ step) for i in range(size)]
            x = x + lax.ppermute(x, axis, pairs)
            step *= 2
    return x


def frame_starts(clip_lengths, total):
    ends = jnp.cumsum(clip_lengths)
    begins = ends - clip_lengths
    index = jnp.arange(total, dtype=jnp.int32)
    chosen = jnp.where(begins[None, :] <= index[:, None], begins[None, :], 0)
    return jnp.max(chosen, axis=1)


def group_moments(field):
    frames, height, width, chans = field.shape
    group_width = chans // GROUPS
    vals = field.astype(jnp.float32).reshape(frames, height * width, GROUPS, group_width)
    sums = jnp.sum(vals, axis=(1, 3))
    squares = jnp.sum(vals * vals, axis=(1, 3))
    both = butterfly_sum(jnp.stack([sums, squares]), ("band", "fsdp"))
    sums, squares = both[0], both[1]
    count = height * width * group_width * lax.axis_size("band") * lax.axis_size("fsdp")
    mean = sums / count
    scale = lax.rsqrt(squares / count - mean * mean + EPS)
    return (mean, scale)


def apply_norm(field, mean, scale, gain):
    shape = field.shape
    chans = shape[-1]
    group_width = chans // GROUPS
    vals = field.astype(jnp.float32).reshape(shape[0], -1, GROUPS, group_width)
    normed = (vals - mean[:, None, :, None]) * scale[:, None, :, None]
    return normed.reshape(shape) * gain


def body(video, clip_lengths, norm_gains, spatial_kernel_weight, w_time, w_qkv, w_out):
    frames, height, width, chans = video.shape
    widths = [w.shape[1] for w in (spatial_kernel_weight, w_time, w_qkv, w_out)]
    packed = jnp.concatenate([spatial_kernel_weight, w_time, w_qkv, w_out], axis=1)
    gathered = lax.all_gather(packed, ("band", "fsdp"), axis=0, tiled=True)
    offsets = [sum(widths[:i]) for i in range(4)]
    space_full, time_full, qkv_full, output_complete = [
        gathered[:, o : o + w] for o, w in zip(offsets, widths)
    ]
    ranks = lax.axis_size("tm")
    total_frames = frames * ranks
    first = lax.axis_index("tm") * frames
    starts = frame_starts(clip_lengths, total_frames)
    local_starts = lax.dynamic_slice_in_dim(starts, first, frames)
    mean_one, scale_one = group_moments(video)
    act = jax.nn.silu(apply_norm(video, mean_one, scale_one, norm_gains[0])).astype(jnp.bfloat16)
    padded = with_halo(act, (("band", 1), ("fsdp", 2)), 1)
    spatial = jnp.zeros((frames, height, width, chans), jnp.float32)
    for tap in range(9):
        shift_y = tap // 3
        shift_x = tap % 3
        spatial = spatial + jnp.einsum(
            "fhwc,cd->fhwd",
            padded[:, shift_y : shift_y + height, shift_x : shift_x + width],
            space_full[:, tap * chans : (tap + 1) * chans],
            preferred_element_type=jnp.float32,
        )
    spatial = spatial.astype(jnp.bfloat16)
    carried = from_behind(spatial[frames - 2 :], "tm", 1)
    extended = jnp.concatenate([carried, spatial], axis=0)
    position = first + jnp.arange(frames, dtype=jnp.int32)
    slots = jnp.arange(frames + 2, dtype=jnp.int32)
    temporal = jnp.zeros((frames, height, width, chans), jnp.float32)
    for tap in range(3):
        source = jnp.maximum(position - 2 + tap, local_starts) - first + 2
        select = (source[:, None] == slots[None, :]).astype(jnp.bfloat16)
        picked = jnp.einsum(
            "fe,ehwc->fhwc", select, extended, preferred_element_type=jnp.float32
        ).astype(jnp.bfloat16)
        temporal = temporal + jnp.einsum(
            "fhwc,cd->fhwd",
            picked,
            time_full[:, tap * chans : (tap + 1) * chans],
            preferred_element_type=jnp.float32,
        )
    resid = (video.astype(jnp.float32) + temporal).astype(jnp.bfloat16)
    pixels = height * width
    group_pixels = pixels // ranks
    flat_resid = resid.reshape(frames, ranks, group_pixels, chans).transpose(1, 0, 2, 3)
    received = lax.all_to_all(flat_resid, "tm", split_axis=0, concat_axis=0, tiled=True)
    resid_time = received.reshape(total_frames, group_pixels, chans)
    mean_two, scale_two = group_moments(resid)
    mine = jnp.concatenate([mean_two, scale_two], axis=1)
    big = jnp.pad(mine, ((0, 8 - frames), (0, 1024 - 2 * GROUPS)))
    moments = lax.all_gather(big, "tm", axis=0, tiled=True).reshape(ranks, 8, 1024)[:, :frames, : 2 * GROUPS]
    moments = moments.reshape(total_frames, 2 * GROUPS)
    mean_all, scale_all = moments[:, :GROUPS], moments[:, GROUPS:]
    flat_norm = apply_norm(resid_time, mean_all, scale_all, norm_gains[1]).astype(jnp.bfloat16)
    qkv_time = jnp.einsum(
        "fpc,cd->fpd", flat_norm, qkv_full, preferred_element_type=jnp.float32
    ).astype(jnp.bfloat16)
    query = qkv_time[..., :chans]
    keys = qkv_time[..., chans : 2 * chans]
    value_rows = qkv_time[..., 2 * chans :]
    index = jnp.arange(total_frames, dtype=jnp.int32)
    allowed = (index[None, :] <= index[:, None]) & (index[None, :] >= starts[:, None])
    scores = jnp.einsum(
        "fpc,gpc->pfg", query, keys, preferred_element_type=jnp.float32
    ) / math.sqrt(chans)
    scores = jnp.where(allowed[None], scores, -1e30)
    top = jnp.max(scores, axis=-1, keepdims=True)
    expo = jnp.where(allowed[None], jnp.exp(scores - top), 0.0)
    attention_probabilities = (expo / jnp.sum(expo, axis=-1, keepdims=True)).astype(jnp.bfloat16)
    attention_output = jnp.einsum(
        "boh,hba->boa", attention_probabilities, value_rows, preferred_element_type=jnp.float32
    ).astype(jnp.bfloat16)
    projected_output = jnp.einsum(
        "axi,iy->axy", attention_output, output_complete, preferred_element_type=jnp.float32
    )
    mixed = (jnp.swapaxes(resid_time, 0, 1).astype(jnp.float32) + projected_output).astype(
        jnp.bfloat16
    )
    return mixed.reshape(1, 1, mixed.shape[0], total_frames, chans)


def solution(mesh):
    return jax.shard_map(
        body,
        mesh=mesh,
        in_specs=(
            P("tm", "band", "fsdp", None),
            P(),
            P(),
            P(("band", "fsdp"), None),
            P(("band", "fsdp"), None),
            P(("band", "fsdp"), None),
            P(("band", "fsdp"), None),
        ),
        out_specs=P("band", "fsdp", "tm", None, None),
        check_vma=False,
    )
```

```python
import math

import jax
import jax.numpy as jnp
from jax import lax
from jax.sharding import PartitionSpec as P

GROUPS = 32


EPS = 1e-06


def with_halo(x, sides, width):
    for axis, dim in sides:
        size, length = (lax.axis_size(axis), x.shape[dim])
        up = [(i, (i + 1) % size) for i in range(size - 1)]
        down = [(j, i) for i, j in up]
        last = lax.slice_in_dim(x, length - width, length, axis=dim)
        initial = lax.slice_in_dim(x, 0, width, axis=dim)
        before = lax.ppermute(last, axis, up)
        after = lax.ppermute(initial, axis, down)
        x = jnp.concatenate([before, x, after], axis=dim)
    return x


def from_behind(x, axis, by):
    length = lax.axis_size(axis)
    pairs = [(i, i + by) for i in range(length) if 0 <= i + by < length]
    return lax.ppermute(x, axis, pairs)


def butterfly_sum(x, axes):
    for axis in axes:
        size = lax.axis_size(axis)
        step = 1
        while step < size:
            pairs = [(i, i ^ step) for i in range(size)]
            x = x + lax.ppermute(x, axis, pairs)
            step *= 2
    return x


def ring_gather(x, axis):
    size = lax.axis_size(axis)
    me = lax.axis_index(axis)
    got = [x]
    for shift in range(1, size):
        got.append(lax.ppermute(x, axis, [(i, (i + shift) % size) for i in range(size)]))
    order = jnp.stack(got[::-1] + got[::-1])
    blocks = lax.dynamic_slice_in_dim(order, (size - 1 - me) % size, size, axis=0)
    return blocks.reshape((size * x.shape[0],) + x.shape[1:])


def frame_starts(clip_lengths, total):
    ends = jnp.cumsum(clip_lengths)
    begins = ends - clip_lengths
    index = jnp.arange(total, dtype=jnp.int32)
    chosen = jnp.where(begins[None, :] <= index[:, None], begins[None, :], 0)
    return jnp.max(chosen, axis=1)


def group_moments(field):
    frames, height, width, chans = field.shape
    group_width = chans // GROUPS
    vals = field.astype(jnp.float32).reshape(frames, height * width, GROUPS, group_width)
    sums = jnp.sum(vals, axis=(1, 3))
    squares = jnp.sum(vals * vals, axis=(1, 3))
    both = butterfly_sum(jnp.stack([sums, squares]), ("band", "fsdp"))
    sums, squares = both[0], both[1]
    count = height * width * group_width * lax.axis_size("band") * lax.axis_size("fsdp")
    mean = sums / count
    scale = lax.rsqrt(squares / count - mean * mean + EPS)
    return (mean, scale)


def apply_norm(field, mean, scale, gain):
    shape = field.shape
    chans = shape[-1]
    group_width = chans // GROUPS
    vals = field.astype(jnp.float32).reshape(shape[0], -1, GROUPS, group_width)
    normed = (vals - mean[:, None, :, None]) * scale[:, None, :, None]
    return normed.reshape(shape) * gain


def body(video, clip_lengths, norm_gains, spatial_kernel_weight, w_time, w_qkv, w_out):
    frames, height, width, chans = video.shape
    widths = [w.shape[1] for w in (spatial_kernel_weight, w_time, w_qkv, w_out)]
    packed = jnp.concatenate([spatial_kernel_weight, w_time, w_qkv, w_out], axis=1)
    gathered = ring_gather(ring_gather(packed, "fsdp"), "band")
    offsets = [sum(widths[:i]) for i in range(4)]
    space_full, time_full, qkv_full, output_complete = [
        gathered[:, o : o + w] for o, w in zip(offsets, widths)
    ]
    ranks = lax.axis_size("tm")
    total_frames = frames * ranks
    first = lax.axis_index("tm") * frames
    starts = frame_starts(clip_lengths, total_frames)
    local_starts = lax.dynamic_slice_in_dim(starts, first, frames)
    mean_one, scale_one = group_moments(video)
    act = jax.nn.silu(apply_norm(video, mean_one, scale_one, norm_gains[0])).astype(jnp.bfloat16)
    padded = with_halo(act, (("band", 1), ("fsdp", 2)), 1)
    spatial = jnp.zeros((frames, height, width, chans), jnp.float32)
    for tap in range(9):
        shift_y = tap // 3
        shift_x = tap % 3
        spatial = spatial + jnp.einsum(
            "fhwc,cd->fhwd",
            padded[:, shift_y : shift_y + height, shift_x : shift_x + width],
            space_full[:, tap * chans : (tap + 1) * chans],
            preferred_element_type=jnp.float32,
        )
    spatial = spatial.astype(jnp.bfloat16)
    carried = from_behind(spatial[frames - 2 :], "tm", 1)
    extended = jnp.concatenate([carried, spatial], axis=0)
    position = first + jnp.arange(frames, dtype=jnp.int32)
    slots = jnp.arange(frames + 2, dtype=jnp.int32)
    temporal = jnp.zeros((frames, height, width, chans), jnp.float32)
    for tap in range(3):
        source = jnp.maximum(position - 2 + tap, local_starts) - first + 2
        select = (source[:, None] == slots[None, :]).astype(jnp.bfloat16)
        picked = jnp.einsum(
            "fe,ehwc->fhwc", select, extended, preferred_element_type=jnp.float32
        ).astype(jnp.bfloat16)
        temporal = temporal + jnp.einsum(
            "fhwc,cd->fhwd",
            picked,
            time_full[:, tap * chans : (tap + 1) * chans],
            preferred_element_type=jnp.float32,
        )
    resid = (video.astype(jnp.float32) + temporal).astype(jnp.bfloat16)
    pixels = height * width
    group_pixels = pixels // ranks
    flat_resid = resid.reshape(frames, ranks, group_pixels, chans).transpose(1, 0, 2, 3)
    received = lax.all_to_all(flat_resid, "tm", split_axis=0, concat_axis=0, tiled=True)
    resid_time = received.reshape(total_frames, group_pixels, chans)
    mean_two, scale_two = group_moments(resid)
    moments = lax.all_gather(
        jnp.concatenate([mean_two, scale_two], axis=1), "tm", axis=0, tiled=True
    )
    mean_all, scale_all = moments[:, :GROUPS], moments[:, GROUPS:]
    flat_norm = apply_norm(resid_time, mean_all, scale_all, norm_gains[1]).astype(jnp.bfloat16)
    qkv_time = jnp.einsum(
        "fpc,cd->fpd", flat_norm, qkv_full, preferred_element_type=jnp.float32
    ).astype(jnp.bfloat16)
    query = qkv_time[..., :chans]
    keys = qkv_time[..., chans : 2 * chans]
    value_rows = qkv_time[..., 2 * chans :]
    index = jnp.arange(total_frames, dtype=jnp.int32)
    allowed = (index[None, :] <= index[:, None]) & (index[None, :] >= starts[:, None])
    scores = jnp.einsum(
        "fpc,gpc->pfg", query, keys, preferred_element_type=jnp.float32
    ) / math.sqrt(chans)
    scores = jnp.where(allowed[None], scores, -1e30)
    top = jnp.max(scores, axis=-1, keepdims=True)
    expo = jnp.where(allowed[None], jnp.exp(scores - top), 0.0)
    attention_probabilities = (expo / jnp.sum(expo, axis=-1, keepdims=True)).astype(jnp.bfloat16)
    attention_output = jnp.einsum(
        "boh,hba->boa", attention_probabilities, value_rows, preferred_element_type=jnp.float32
    ).astype(jnp.bfloat16)
    projected_output = jnp.einsum(
        "axi,iy->axy", attention_output, output_complete, preferred_element_type=jnp.float32
    )
    mixed = (jnp.swapaxes(resid_time, 0, 1).astype(jnp.float32) + projected_output).astype(
        jnp.bfloat16
    )
    return mixed.reshape(1, 1, mixed.shape[0], total_frames, chans)


def solution(mesh):
    return jax.shard_map(
        body,
        mesh=mesh,
        in_specs=(
            P("tm", "band", "fsdp", None),
            P(),
            P(),
            P(("band", "fsdp"), None),
            P(("band", "fsdp"), None),
            P(("band", "fsdp"), None),
            P(("band", "fsdp"), None),
        ),
        out_specs=P("band", "fsdp", "tm", None, None),
        check_vma=False,
    )
```

```python
import math

import jax
import jax.numpy as jnp
from jax import lax
from jax.sharding import Mesh
from jax.sharding import PartitionSpec as P


GROUPS = 32
TM = ("z", "core")


EPS = 1e-06


def with_halo(x, sides, width):
    for axis, dim in sides:
        size, length = (lax.axis_size(axis), x.shape[dim])
        up = [(i, (i + 1) % size) for i in range(size - 1)]
        down = [(j, i) for i, j in up]
        last = lax.slice_in_dim(x, length - width, length, axis=dim)
        initial = lax.slice_in_dim(x, 0, width, axis=dim)
        before = lax.ppermute(last, axis, up)
        after = lax.ppermute(initial, axis, down)
        x = jnp.concatenate([before, x, after], axis=dim)
    return x


def from_behind(x, axis, by):
    length = lax.axis_size(axis)
    pairs = [(i, i + by) for i in range(length) if 0 <= i + by < length]
    return lax.ppermute(x, axis, pairs)


def butterfly_sum(x, axes):
    for axis in axes:
        size = lax.axis_size(axis)
        step = 1
        while step < size:
            pairs = [(i, i ^ step) for i in range(size)]
            x = x + lax.ppermute(x, axis, pairs)
            step *= 2
    return x


def ring_gather(x, axis):
    size = lax.axis_size(axis)
    me = lax.axis_index(axis)
    got = [x]
    for shift in range(1, size):
        got.append(lax.ppermute(x, axis, [(i, (i + shift) % size) for i in range(size)]))
    order = jnp.stack(got[::-1] + got[::-1])
    blocks = lax.dynamic_slice_in_dim(order, (size - 1 - me) % size, size, axis=0)
    return blocks.reshape((size * x.shape[0],) + x.shape[1:])


def frame_starts(clip_lengths, total):
    ends = jnp.cumsum(clip_lengths)
    begins = ends - clip_lengths
    index = jnp.arange(total, dtype=jnp.int32)
    chosen = jnp.where(begins[None, :] <= index[:, None], begins[None, :], 0)
    return jnp.max(chosen, axis=1)


def group_moments(field):
    frames, height, width, chans = field.shape
    group_width = chans // GROUPS
    vals = field.astype(jnp.float32).reshape(frames, height * width, GROUPS, group_width)
    sums = jnp.sum(vals, axis=(1, 3))
    squares = jnp.sum(vals * vals, axis=(1, 3))
    both = butterfly_sum(jnp.stack([sums, squares]), ("band", "fsdp"))
    sums, squares = both[0], both[1]
    count = height * width * group_width * lax.axis_size("band") * lax.axis_size("fsdp")
    mean = sums / count
    scale = lax.rsqrt(squares / count - mean * mean + EPS)
    return (mean, scale)


def apply_norm(field, mean, scale, gain):
    shape = field.shape
    chans = shape[-1]
    group_width = chans // GROUPS
    vals = field.astype(jnp.float32).reshape(shape[0], -1, GROUPS, group_width)
    normed = (vals - mean[:, None, :, None]) * scale[:, None, :, None]
    return normed.reshape(shape) * gain


def body(video, clip_lengths, norm_gains, spatial_kernel_weight, w_time, w_qkv, w_out):
    frames, height, width, chans = video.shape
    widths = [w.shape[1] for w in (spatial_kernel_weight, w_time, w_qkv, w_out)]
    packed = jnp.concatenate([spatial_kernel_weight, w_time, w_qkv, w_out], axis=1)
    first_stage = ring_gather(packed, "fsdp")
    gathered = ring_gather(first_stage, "band")
    offsets = [sum(widths[:i]) for i in range(4)]
    space_full, time_full, qkv_full, output_complete = [
        gathered[:, o : o + w] for o, w in zip(offsets, widths)
    ]
    ranks = lax.axis_size(TM)
    total_frames = frames * ranks
    first = lax.axis_index(TM) * frames
    starts = frame_starts(clip_lengths, total_frames)
    local_starts = lax.dynamic_slice_in_dim(starts, first, frames)
    mean_one, scale_one = group_moments(video)
    act = jax.nn.silu(apply_norm(video, mean_one, scale_one, norm_gains[0])).astype(jnp.bfloat16)
    padded = with_halo(act, (("band", 1), ("fsdp", 2)), 1)
    spatial = jnp.zeros((frames, height, width, chans), jnp.float32)
    for tap in range(9):
        shift_y = tap // 3
        shift_x = tap % 3
        spatial = spatial + jnp.einsum(
            "fhwc,cd->fhwd",
            padded[:, shift_y : shift_y + height, shift_x : shift_x + width],
            space_full[:, tap * chans : (tap + 1) * chans],
            preferred_element_type=jnp.float32,
        )
    spatial = spatial.astype(jnp.bfloat16)
    carried = from_behind(spatial[frames - 2 :], TM, 1)
    extended = jnp.concatenate([carried, spatial], axis=0)
    position = first + jnp.arange(frames, dtype=jnp.int32)
    slots = jnp.arange(frames + 2, dtype=jnp.int32)
    temporal = jnp.zeros((frames, height, width, chans), jnp.float32)
    for tap in range(3):
        source = jnp.maximum(position - 2 + tap, local_starts) - first + 2
        select = (source[:, None] == slots[None, :]).astype(jnp.bfloat16)
        picked = jnp.einsum(
            "fe,ehwc->fhwc", select, extended, preferred_element_type=jnp.float32
        ).astype(jnp.bfloat16)
        temporal = temporal + jnp.einsum(
            "fhwc,cd->fhwd",
            picked,
            time_full[:, tap * chans : (tap + 1) * chans],
            preferred_element_type=jnp.float32,
        )
    resid = (video.astype(jnp.float32) + temporal).astype(jnp.bfloat16)
    pixels = height * width
    group_pixels = pixels // ranks
    flat_resid = resid.reshape(frames, ranks, group_pixels, chans).transpose(1, 0, 2, 3)
    received = lax.all_to_all(flat_resid, TM, split_axis=0, concat_axis=0, tiled=True)
    resid_time = received.reshape(total_frames, group_pixels, chans)
    mean_two, scale_two = group_moments(resid)
    moments = jnp.concatenate([mean_two, scale_two], axis=1)
    for axis in TM[::-1]:
        moments = lax.all_gather(moments, axis, axis=0, tiled=True)
    mean_all, scale_all = moments[:, :GROUPS], moments[:, GROUPS:]
    flat_norm = apply_norm(resid_time, mean_all, scale_all, norm_gains[1]).astype(jnp.bfloat16)
    qkv_time = jnp.einsum(
        "fpc,cd->fpd", flat_norm, qkv_full, preferred_element_type=jnp.float32
    ).astype(jnp.bfloat16)
    query = qkv_time[..., :chans]
    keys = qkv_time[..., chans : 2 * chans]
    value_rows = qkv_time[..., 2 * chans :]
    index = jnp.arange(total_frames, dtype=jnp.int32)
    allowed = (index[None, :] <= index[:, None]) & (index[None, :] >= starts[:, None])
    scores = jnp.einsum(
        "fpc,gpc->pfg", query, keys, preferred_element_type=jnp.float32
    ) / math.sqrt(chans)
    scores = jnp.where(allowed[None], scores, -1e30)
    top = jnp.max(scores, axis=-1, keepdims=True)
    expo = jnp.where(allowed[None], jnp.exp(scores - top), 0.0)
    attention_probabilities = (expo / jnp.sum(expo, axis=-1, keepdims=True)).astype(jnp.bfloat16)
    attention_output = jnp.einsum(
        "boh,hba->boa", attention_probabilities, value_rows, preferred_element_type=jnp.float32
    ).astype(jnp.bfloat16)
    projected_output = jnp.einsum(
        "axi,iy->axy", attention_output, output_complete, preferred_element_type=jnp.float32
    )
    mixed = (jnp.swapaxes(resid_time, 0, 1).astype(jnp.float32) + projected_output).astype(
        jnp.bfloat16
    )
    return mixed.reshape(1, 1, mixed.shape[0], total_frames, chans)


def solution(mesh):
    devices = mesh.devices
    split = Mesh(
        devices.reshape((devices.shape[0] // 2, 2) + devices.shape[1:]),
        ("z", "core", "band", "fsdp"),
    )
    return jax.shard_map(
        body,
        mesh=split,
        in_specs=(
            P(TM, "band", "fsdp", None),
            P(),
            P(),
            P(("band", "fsdp"), None),
            P(("band", "fsdp"), None),
            P(("band", "fsdp"), None),
            P(("band", "fsdp"), None),
        ),
        out_specs=P("band", "fsdp", TM, None, None),
        check_vma=False,
    )
```

```python
import math

import jax
import jax.numpy as jnp
from jax import lax
from jax.sharding import Mesh
from jax.sharding import PartitionSpec as P


GROUPS = 32
TM = ("z", "core")


EPS = 1e-06


def with_halo(x, sides, width):
    for axis, dim in sides:
        size, length = (lax.axis_size(axis), x.shape[dim])
        up = [(i, (i + 1) % size) for i in range(size - 1)]
        down = [(j, i) for i, j in up]
        last = lax.slice_in_dim(x, length - width, length, axis=dim)
        initial = lax.slice_in_dim(x, 0, width, axis=dim)
        before = lax.ppermute(last, axis, up)
        after = lax.ppermute(initial, axis, down)
        x = jnp.concatenate([before, x, after], axis=dim)
    return x


def from_behind(x, axis, by):
    length = lax.axis_size(axis)
    pairs = [(i, i + by) for i in range(length) if 0 <= i + by < length]
    return lax.ppermute(x, axis, pairs)


def butterfly_sum(x, axes):
    for axis in axes:
        size = lax.axis_size(axis)
        step = 1
        while step < size:
            pairs = [(i, i ^ step) for i in range(size)]
            x = x + lax.ppermute(x, axis, pairs)
            step *= 2
    return x


def ring_gather(x, axis):
    size = lax.axis_size(axis)
    me = lax.axis_index(axis)
    got = [x]
    for shift in range(1, size):
        got.append(lax.ppermute(x, axis, [(i, (i + shift) % size) for i in range(size)]))
    order = jnp.stack(got[::-1] + got[::-1])
    blocks = lax.dynamic_slice_in_dim(order, (size - 1 - me) % size, size, axis=0)
    return blocks.reshape((size * x.shape[0],) + x.shape[1:])


def frame_starts(clip_lengths, total):
    ends = jnp.cumsum(clip_lengths)
    begins = ends - clip_lengths
    index = jnp.arange(total, dtype=jnp.int32)
    chosen = jnp.where(begins[None, :] <= index[:, None], begins[None, :], 0)
    return jnp.max(chosen, axis=1)


def group_moments(field):
    frames, height, width, chans = field.shape
    group_width = chans // GROUPS
    vals = field.astype(jnp.float32).reshape(frames, height * width, GROUPS, group_width)
    sums = jnp.sum(vals, axis=(1, 3))
    squares = jnp.sum(vals * vals, axis=(1, 3))
    both = butterfly_sum(jnp.stack([sums, squares]), ("band", "fsdp"))
    sums, squares = both[0], both[1]
    count = height * width * group_width * lax.axis_size("band") * lax.axis_size("fsdp")
    mean = sums / count
    scale = lax.rsqrt(squares / count - mean * mean + EPS)
    return (mean, scale)


def apply_norm(field, mean, scale, gain):
    shape = field.shape
    chans = shape[-1]
    group_width = chans // GROUPS
    vals = field.astype(jnp.float32).reshape(shape[0], -1, GROUPS, group_width)
    normed = (vals - mean[:, None, :, None]) * scale[:, None, :, None]
    return normed.reshape(shape) * gain


def body(video, clip_lengths, norm_gains, spatial_kernel_weight, w_time, w_qkv, w_out):
    frames, height, width, chans = video.shape
    widths = [w.shape[1] for w in (spatial_kernel_weight, w_time, w_qkv, w_out)]
    packed = jnp.concatenate([spatial_kernel_weight, w_time, w_qkv, w_out], axis=1)
    half = packed.shape[1] // 2
    core = lax.axis_index("core")
    mine = lax.dynamic_slice_in_dim(packed, core * half, half, axis=1)
    first_stage = ring_gather(mine, "fsdp")
    second_stage = ring_gather(first_stage, "band")
    other = lax.ppermute(second_stage, "core", [(0, 1), (1, 0)])
    both = jnp.stack([second_stage, other, second_stage])
    gathered = jnp.concatenate(
        [lax.dynamic_index_in_dim(both, core, 0, keepdims=False),
         lax.dynamic_index_in_dim(both, core + 1, 0, keepdims=False)],
        axis=1,
    )
    offsets = [sum(widths[:i]) for i in range(4)]
    space_full, time_full, qkv_full, output_complete = [
        gathered[:, o : o + w] for o, w in zip(offsets, widths)
    ]
    ranks = lax.axis_size(TM)
    total_frames = frames * ranks
    first = lax.axis_index(TM) * frames
    starts = frame_starts(clip_lengths, total_frames)
    local_starts = lax.dynamic_slice_in_dim(starts, first, frames)
    mean_one, scale_one = group_moments(video)
    act = jax.nn.silu(apply_norm(video, mean_one, scale_one, norm_gains[0])).astype(jnp.bfloat16)
    padded = with_halo(act, (("band", 1), ("fsdp", 2)), 1)
    spatial = jnp.zeros((frames, height, width, chans), jnp.float32)
    for tap in range(9):
        shift_y = tap // 3
        shift_x = tap % 3
        spatial = spatial + jnp.einsum(
            "fhwc,cd->fhwd",
            padded[:, shift_y : shift_y + height, shift_x : shift_x + width],
            space_full[:, tap * chans : (tap + 1) * chans],
            preferred_element_type=jnp.float32,
        )
    spatial = spatial.astype(jnp.bfloat16)
    carried = from_behind(spatial[frames - 2 :], TM, 1)
    extended = jnp.concatenate([carried, spatial], axis=0)
    position = first + jnp.arange(frames, dtype=jnp.int32)
    slots = jnp.arange(frames + 2, dtype=jnp.int32)
    temporal = jnp.zeros((frames, height, width, chans), jnp.float32)
    for tap in range(3):
        source = jnp.maximum(position - 2 + tap, local_starts) - first + 2
        select = (source[:, None] == slots[None, :]).astype(jnp.bfloat16)
        picked = jnp.einsum(
            "fe,ehwc->fhwc", select, extended, preferred_element_type=jnp.float32
        ).astype(jnp.bfloat16)
        temporal = temporal + jnp.einsum(
            "fhwc,cd->fhwd",
            picked,
            time_full[:, tap * chans : (tap + 1) * chans],
            preferred_element_type=jnp.float32,
        )
    resid = (video.astype(jnp.float32) + temporal).astype(jnp.bfloat16)
    pixels = height * width
    group_pixels = pixels // ranks
    flat_resid = resid.reshape(frames, ranks, group_pixels, chans).transpose(1, 0, 2, 3)
    received = lax.all_to_all(flat_resid, TM, split_axis=0, concat_axis=0, tiled=True)
    resid_time = received.reshape(total_frames, group_pixels, chans)
    mean_two, scale_two = group_moments(resid)
    moments = jnp.concatenate([mean_two, scale_two], axis=1)
    for axis in TM[::-1]:
        moments = lax.all_gather(moments, axis, axis=0, tiled=True)
    mean_all, scale_all = moments[:, :GROUPS], moments[:, GROUPS:]
    flat_norm = apply_norm(resid_time, mean_all, scale_all, norm_gains[1]).astype(jnp.bfloat16)
    qkv_time = jnp.einsum(
        "fpc,cd->fpd", flat_norm, qkv_full, preferred_element_type=jnp.float32
    ).astype(jnp.bfloat16)
    query = qkv_time[..., :chans]
    keys = qkv_time[..., chans : 2 * chans]
    value_rows = qkv_time[..., 2 * chans :]
    index = jnp.arange(total_frames, dtype=jnp.int32)
    allowed = (index[None, :] <= index[:, None]) & (index[None, :] >= starts[:, None])
    scores = jnp.einsum(
        "fpc,gpc->pfg", query, keys, preferred_element_type=jnp.float32
    ) / math.sqrt(chans)
    scores = jnp.where(allowed[None], scores, -1e30)
    top = jnp.max(scores, axis=-1, keepdims=True)
    expo = jnp.where(allowed[None], jnp.exp(scores - top), 0.0)
    attention_probabilities = (expo / jnp.sum(expo, axis=-1, keepdims=True)).astype(jnp.bfloat16)
    attention_output = jnp.einsum(
        "boh,hba->boa", attention_probabilities, value_rows, preferred_element_type=jnp.float32
    ).astype(jnp.bfloat16)
    projected_output = jnp.einsum(
        "axi,iy->axy", attention_output, output_complete, preferred_element_type=jnp.float32
    )
    mixed = (jnp.swapaxes(resid_time, 0, 1).astype(jnp.float32) + projected_output).astype(
        jnp.bfloat16
    )
    return mixed.reshape(1, 1, mixed.shape[0], total_frames, chans)


def solution(mesh):
    devices = mesh.devices
    split = Mesh(
        devices.reshape((devices.shape[0] // 2, 2) + devices.shape[1:]),
        ("z", "core", "band", "fsdp"),
    )
    return jax.shard_map(
        body,
        mesh=split,
        in_specs=(
            P(TM, "band", "fsdp", None),
            P(),
            P(),
            P(("band", "fsdp"), None),
            P(("band", "fsdp"), None),
            P(("band", "fsdp"), None),
            P(("band", "fsdp"), None),
        ),
        out_specs=P("band", "fsdp", TM, None, None),
        check_vma=False,
    )
```

```python
import math

import jax
import jax.numpy as jnp
from jax import lax
from jax.sharding import Mesh
from jax.sharding import PartitionSpec as P


GROUPS = 32
TM = ("z", "core")


EPS = 1e-06


def with_halo(x, sides, width):
    for axis, dim in sides:
        size, length = (lax.axis_size(axis), x.shape[dim])
        up = [(i, (i + 1) % size) for i in range(size - 1)]
        down = [(j, i) for i, j in up]
        last = lax.slice_in_dim(x, length - width, length, axis=dim)
        initial = lax.slice_in_dim(x, 0, width, axis=dim)
        before = lax.ppermute(last, axis, up)
        after = lax.ppermute(initial, axis, down)
        x = jnp.concatenate([before, x, after], axis=dim)
    return x


def from_behind(x, axis, by):
    length = lax.axis_size(axis)
    pairs = [(i, i + by) for i in range(length) if 0 <= i + by < length]
    return lax.ppermute(x, axis, pairs)


def butterfly_sum(x, axes):
    for axis in axes:
        size = lax.axis_size(axis)
        step = 1
        while step < size:
            pairs = [(i, i ^ step) for i in range(size)]
            x = x + lax.ppermute(x, axis, pairs)
            step *= 2
    return x


def ring_gather(x, axis):
    size = lax.axis_size(axis)
    me = lax.axis_index(axis)
    got = [x]
    for shift in range(1, size):
        got.append(lax.ppermute(x, axis, [(i, (i + shift) % size) for i in range(size)]))
    order = jnp.stack(got[::-1] + got[::-1])
    blocks = lax.dynamic_slice_in_dim(order, (size - 1 - me) % size, size, axis=0)
    return blocks.reshape((size * x.shape[0],) + x.shape[1:])


def frame_starts(clip_lengths, total):
    ends = jnp.cumsum(clip_lengths)
    begins = ends - clip_lengths
    index = jnp.arange(total, dtype=jnp.int32)
    chosen = jnp.where(begins[None, :] <= index[:, None], begins[None, :], 0)
    return jnp.max(chosen, axis=1)


def group_moments(field):
    frames, height, width, chans = field.shape
    group_width = chans // GROUPS
    vals = field.astype(jnp.float32).reshape(frames, height * width, GROUPS, group_width)
    sums = jnp.sum(vals, axis=(1, 3))
    squares = jnp.sum(vals * vals, axis=(1, 3))
    both = butterfly_sum(jnp.stack([sums, squares]), ("band", "fsdp"))
    sums, squares = both[0], both[1]
    count = height * width * group_width * lax.axis_size("band") * lax.axis_size("fsdp")
    mean = sums / count
    scale = lax.rsqrt(squares / count - mean * mean + EPS)
    return (mean, scale)


def apply_norm(field, mean, scale, gain):
    shape = field.shape
    chans = shape[-1]
    group_width = chans // GROUPS
    vals = field.astype(jnp.float32).reshape(shape[0], -1, GROUPS, group_width)
    normed = (vals - mean[:, None, :, None]) * scale[:, None, :, None]
    return normed.reshape(shape) * gain


def body(video, clip_lengths, norm_gains, spatial_kernel_weight, w_time, w_qkv, w_out):
    frames, height, width, chans = video.shape
    widths = [w.shape[1] for w in (spatial_kernel_weight, w_time, w_qkv, w_out)]
    packed = jnp.concatenate([spatial_kernel_weight, w_time, w_qkv, w_out], axis=1)
    half = packed.shape[1] // 2
    core = lax.axis_index("core")
    mine = lax.dynamic_slice_in_dim(packed, core * half, half, axis=1)
    first_stage = ring_gather(mine, "fsdp")
    second_stage = ring_gather(first_stage, "band")
    other = lax.ppermute(second_stage, "core", [(0, 1), (1, 0)])
    both = jnp.stack([second_stage, other, second_stage])
    gathered = jnp.concatenate(
        [lax.dynamic_index_in_dim(both, core, 0, keepdims=False),
         lax.dynamic_index_in_dim(both, core + 1, 0, keepdims=False)],
        axis=1,
    )
    offsets = [sum(widths[:i]) for i in range(4)]
    space_full, time_full, qkv_full, output_complete = [
        gathered[:, o : o + w] for o, w in zip(offsets, widths)
    ]
    ranks = lax.axis_size(TM)
    total_frames = frames * ranks
    first = lax.axis_index(TM) * frames
    starts = frame_starts(clip_lengths, total_frames)
    local_starts = lax.dynamic_slice_in_dim(starts, first, frames)
    mean_one, scale_one = group_moments(video)
    act = jax.nn.silu(apply_norm(video, mean_one, scale_one, norm_gains[0])).astype(jnp.bfloat16)
    padded = with_halo(act, (("band", 1), ("fsdp", 2)), 1)
    spatial = jnp.zeros((frames, height, width, chans), jnp.float32)
    for tap in range(9):
        shift_y = tap // 3
        shift_x = tap % 3
        spatial = spatial + jnp.einsum(
            "fhwc,cd->fhwd",
            padded[:, shift_y : shift_y + height, shift_x : shift_x + width],
            space_full[:, tap * chans : (tap + 1) * chans],
            preferred_element_type=jnp.float32,
        )
    spatial = spatial.astype(jnp.bfloat16)
    carried = from_behind(spatial[frames - 2 :], TM, 1)
    extended = jnp.concatenate([carried, spatial], axis=0)
    position = first + jnp.arange(frames, dtype=jnp.int32)
    slots = jnp.arange(frames + 2, dtype=jnp.int32)
    temporal = jnp.zeros((frames, height, width, chans), jnp.float32)
    for tap in range(3):
        source = jnp.maximum(position - 2 + tap, local_starts) - first + 2
        select = (source[:, None] == slots[None, :]).astype(jnp.bfloat16)
        picked = jnp.einsum(
            "fe,ehwc->fhwc", select, extended, preferred_element_type=jnp.float32
        ).astype(jnp.bfloat16)
        temporal = temporal + jnp.einsum(
            "fhwc,cd->fhwd",
            picked,
            time_full[:, tap * chans : (tap + 1) * chans],
            preferred_element_type=jnp.float32,
        )
    resid = (video.astype(jnp.float32) + temporal).astype(jnp.bfloat16)
    pixels = height * width
    flat_resid = resid.reshape(frames, pixels, chans)
    resid_time = lax.all_to_all(flat_resid, TM, split_axis=1, concat_axis=0, tiled=True)
    mean_two, scale_two = group_moments(resid)
    moments = jnp.concatenate([mean_two, scale_two], axis=1)
    for axis in TM[::-1]:
        moments = lax.all_gather(moments, axis, axis=0, tiled=True)
    mean_all, scale_all = moments[:, :GROUPS], moments[:, GROUPS:]
    flat_norm = apply_norm(resid_time, mean_all, scale_all, norm_gains[1]).astype(jnp.bfloat16)
    qkv_time = jnp.einsum(
        "fpc,cd->fpd", flat_norm, qkv_full, preferred_element_type=jnp.float32
    ).astype(jnp.bfloat16)
    query = qkv_time[..., :chans]
    keys = qkv_time[..., chans : 2 * chans]
    value_rows = qkv_time[..., 2 * chans :]
    index = jnp.arange(total_frames, dtype=jnp.int32)
    allowed = (index[None, :] <= index[:, None]) & (index[None, :] >= starts[:, None])
    scores = jnp.einsum(
        "fpc,gpc->pfg", query, keys, preferred_element_type=jnp.float32
    ) / math.sqrt(chans)
    scores = jnp.where(allowed[None], scores, -1e30)
    top = jnp.max(scores, axis=-1, keepdims=True)
    expo = jnp.where(allowed[None], jnp.exp(scores - top), 0.0)
    attention_probabilities = (expo / jnp.sum(expo, axis=-1, keepdims=True)).astype(jnp.bfloat16)
    attention_output = jnp.einsum(
        "boh,hba->boa", attention_probabilities, value_rows, preferred_element_type=jnp.float32
    ).astype(jnp.bfloat16)
    projected_output = jnp.einsum(
        "axi,iy->axy", attention_output, output_complete, preferred_element_type=jnp.float32
    )
    mixed = (jnp.swapaxes(resid_time, 0, 1).astype(jnp.float32) + projected_output).astype(
        jnp.bfloat16
    )
    return mixed.reshape(1, 1, mixed.shape[0], total_frames, chans)


def solution(mesh):
    devices = mesh.devices
    split = Mesh(
        devices.reshape((devices.shape[0] // 2, 2) + devices.shape[1:]),
        ("z", "core", "band", "fsdp"),
    )
    return jax.shard_map(
        body,
        mesh=split,
        in_specs=(
            P(TM, "band", "fsdp", None),
            P(),
            P(),
            P(("band", "fsdp"), None),
            P(("band", "fsdp"), None),
            P(("band", "fsdp"), None),
            P(("band", "fsdp"), None),
        ),
        out_specs=P("band", "fsdp", TM, None, None),
        check_vma=False,
    )
```

```python
import math

import jax
import jax.numpy as jnp
from jax import lax
from jax.sharding import Mesh
from jax.sharding import PartitionSpec as P


GROUPS = 32
TM = ("z", "core")


EPS = 1e-06


def with_halo(x, sides, width):
    for axis, dim in sides:
        size, length = (lax.axis_size(axis), x.shape[dim])
        up = [(i, (i + 1) % size) for i in range(size - 1)]
        down = [(j, i) for i, j in up]
        last = lax.slice_in_dim(x, length - width, length, axis=dim)
        initial = lax.slice_in_dim(x, 0, width, axis=dim)
        before = lax.ppermute(last, axis, up)
        after = lax.ppermute(initial, axis, down)
        x = jnp.concatenate([before, x, after], axis=dim)
    return x


def from_behind(x, axis, by):
    length = lax.axis_size(axis)
    pairs = [(i, i + by) for i in range(length) if 0 <= i + by < length]
    return lax.ppermute(x, axis, pairs)


def ring_gather(x, axis):
    size = lax.axis_size(axis)
    me = lax.axis_index(axis)
    got = [x]
    for shift in range(1, size):
        got.append(lax.ppermute(x, axis, [(i, (i + shift) % size) for i in range(size)]))
    order = jnp.stack(got[::-1] + got[::-1])
    blocks = lax.dynamic_slice_in_dim(order, (size - 1 - me) % size, size, axis=0)
    return blocks.reshape((size * x.shape[0],) + x.shape[1:])


def frame_starts(clip_lengths, total):
    ends = jnp.cumsum(clip_lengths)
    begins = ends - clip_lengths
    index = jnp.arange(total, dtype=jnp.int32)
    chosen = jnp.where(begins[None, :] <= index[:, None], begins[None, :], 0)
    return jnp.max(chosen, axis=1)


def group_moments(field):
    frames, height, width, chans = field.shape
    group_width = chans // GROUPS
    vals = field.astype(jnp.float32).reshape(frames, height * width, GROUPS, group_width)
    sums = jnp.sum(vals, axis=(1, 3))
    squares = jnp.sum(vals * vals, axis=(1, 3))
    both = lax.psum(jnp.stack([sums, squares]), "band")
    both = lax.psum(lax.optimization_barrier(both), "fsdp")
    sums, squares = both[0], both[1]
    count = height * width * group_width * lax.axis_size("band") * lax.axis_size("fsdp")
    mean = sums / count
    scale = lax.rsqrt(squares / count - mean * mean + EPS)
    return (mean, scale)


def apply_norm(field, mean, scale, gain):
    shape = field.shape
    chans = shape[-1]
    group_width = chans // GROUPS
    vals = field.astype(jnp.float32).reshape(shape[0], -1, GROUPS, group_width)
    normed = (vals - mean[:, None, :, None]) * scale[:, None, :, None]
    return normed.reshape(shape) * gain


def body(video, clip_lengths, norm_gains, spatial_kernel_weight, w_time, w_qkv, w_out):
    frames, height, width, chans = video.shape
    widths = [w.shape[1] for w in (spatial_kernel_weight, w_time, w_qkv, w_out)]
    packed = jnp.concatenate([spatial_kernel_weight, w_time, w_qkv, w_out], axis=1)
    half = packed.shape[1] // 2
    core = lax.axis_index("core")
    mine = lax.dynamic_slice_in_dim(packed, core * half, half, axis=1)
    first_stage = ring_gather(mine, "fsdp")
    second_stage = ring_gather(first_stage, "band")
    other = lax.ppermute(second_stage, "core", [(0, 1), (1, 0)])
    both = jnp.stack([second_stage, other, second_stage])
    gathered = jnp.concatenate(
        [lax.dynamic_index_in_dim(both, core, 0, keepdims=False),
         lax.dynamic_index_in_dim(both, core + 1, 0, keepdims=False)],
        axis=1,
    )
    offsets = [sum(widths[:i]) for i in range(4)]
    space_full, time_full, qkv_full, output_complete = [
        gathered[:, o : o + w] for o, w in zip(offsets, widths)
    ]
    ranks = lax.axis_size(TM)
    total_frames = frames * ranks
    first = lax.axis_index(TM) * frames
    starts = frame_starts(clip_lengths, total_frames)
    local_starts = lax.dynamic_slice_in_dim(starts, first, frames)
    mean_one, scale_one = group_moments(video)
    act = jax.nn.silu(apply_norm(video, mean_one, scale_one, norm_gains[0])).astype(jnp.bfloat16)
    padded = with_halo(act, (("band", 1), ("fsdp", 2)), 1)
    spatial = jnp.zeros((frames, height, width, chans), jnp.float32)
    for tap in range(9):
        shift_y = tap // 3
        shift_x = tap % 3
        spatial = spatial + jnp.einsum(
            "fhwc,cd->fhwd",
            padded[:, shift_y : shift_y + height, shift_x : shift_x + width],
            space_full[:, tap * chans : (tap + 1) * chans],
            preferred_element_type=jnp.float32,
        )
    spatial = spatial.astype(jnp.bfloat16)
    carried = from_behind(spatial[frames - 2 :], TM, 1)
    extended = jnp.concatenate([carried, spatial], axis=0)
    position = first + jnp.arange(frames, dtype=jnp.int32)
    slots = jnp.arange(frames + 2, dtype=jnp.int32)
    temporal = jnp.zeros((frames, height, width, chans), jnp.float32)
    for tap in range(3):
        source = jnp.maximum(position - 2 + tap, local_starts) - first + 2
        select = (source[:, None] == slots[None, :]).astype(jnp.bfloat16)
        picked = jnp.einsum(
            "fe,ehwc->fhwc", select, extended, preferred_element_type=jnp.float32
        ).astype(jnp.bfloat16)
        temporal = temporal + jnp.einsum(
            "fhwc,cd->fhwd",
            picked,
            time_full[:, tap * chans : (tap + 1) * chans],
            preferred_element_type=jnp.float32,
        )
    resid = (video.astype(jnp.float32) + temporal).astype(jnp.bfloat16)
    pixels = height * width
    group_pixels = pixels // ranks
    flat_resid = resid.reshape(frames, ranks, group_pixels, chans).transpose(1, 0, 2, 3)
    received = lax.all_to_all(flat_resid, TM, split_axis=0, concat_axis=0, tiled=True)
    resid_time = received.reshape(total_frames, group_pixels, chans)
    mean_two, scale_two = group_moments(resid)
    moments = jnp.concatenate([mean_two, scale_two], axis=1)
    for axis in TM[::-1]:
        moments = lax.all_gather(moments, axis, axis=0, tiled=True)
    mean_all, scale_all = moments[:, :GROUPS], moments[:, GROUPS:]
    flat_norm = apply_norm(resid_time, mean_all, scale_all, norm_gains[1]).astype(jnp.bfloat16)
    qkv_time = jnp.einsum(
        "fpc,cd->fpd", flat_norm, qkv_full, preferred_element_type=jnp.float32
    ).astype(jnp.bfloat16)
    query = qkv_time[..., :chans]
    keys = qkv_time[..., chans : 2 * chans]
    value_rows = qkv_time[..., 2 * chans :]
    index = jnp.arange(total_frames, dtype=jnp.int32)
    allowed = (index[None, :] <= index[:, None]) & (index[None, :] >= starts[:, None])
    scores = jnp.einsum(
        "fpc,gpc->pfg", query, keys, preferred_element_type=jnp.float32
    ) / math.sqrt(chans)
    scores = jnp.where(allowed[None], scores, -1e30)
    top = jnp.max(scores, axis=-1, keepdims=True)
    expo = jnp.where(allowed[None], jnp.exp(scores - top), 0.0)
    attention_probabilities = (expo / jnp.sum(expo, axis=-1, keepdims=True)).astype(jnp.bfloat16)
    attention_output = jnp.einsum(
        "boh,hba->boa", attention_probabilities, value_rows, preferred_element_type=jnp.float32
    ).astype(jnp.bfloat16)
    projected_output = jnp.einsum(
        "axi,iy->axy", attention_output, output_complete, preferred_element_type=jnp.float32
    )
    mixed = (jnp.swapaxes(resid_time, 0, 1).astype(jnp.float32) + projected_output).astype(
        jnp.bfloat16
    )
    return mixed.reshape(1, 1, mixed.shape[0], total_frames, chans)


def solution(mesh):
    devices = mesh.devices
    split = Mesh(
        devices.reshape((devices.shape[0] // 2, 2) + devices.shape[1:]),
        ("z", "core", "band", "fsdp"),
    )
    return jax.shard_map(
        body,
        mesh=split,
        in_specs=(
            P(TM, "band", "fsdp", None),
            P(),
            P(),
            P(("band", "fsdp"), None),
            P(("band", "fsdp"), None),
            P(("band", "fsdp"), None),
            P(("band", "fsdp"), None),
        ),
        out_specs=P("band", "fsdp", TM, None, None),
        check_vma=False,
    )
```

```python
import math

import jax
import jax.numpy as jnp
from jax import lax
from jax.sharding import Mesh
from jax.sharding import PartitionSpec as P


GROUPS = 32
TM = ("zh", "zl", "core")


EPS = 1e-06


def with_halo(x, sides, width):
    for axis, dim in sides:
        size, length = (lax.axis_size(axis), x.shape[dim])
        up = [(i, (i + 1) % size) for i in range(size - 1)]
        down = [(j, i) for i, j in up]
        last = lax.slice_in_dim(x, length - width, length, axis=dim)
        initial = lax.slice_in_dim(x, 0, width, axis=dim)
        before = lax.ppermute(last, axis, up)
        after = lax.ppermute(initial, axis, down)
        x = jnp.concatenate([before, x, after], axis=dim)
    return x


def from_behind(x, axis, by):
    length = lax.axis_size(axis)
    pairs = [(i, i + by) for i in range(length) if 0 <= i + by < length]
    return lax.ppermute(x, axis, pairs)


def ring_gather(x, axis):
    size = lax.axis_size(axis)
    me = lax.axis_index(axis)
    got = [x]
    for shift in range(1, size):
        got.append(lax.ppermute(x, axis, [(i, (i + shift) % size) for i in range(size)]))
    order = jnp.stack(got[::-1] + got[::-1])
    blocks = lax.dynamic_slice_in_dim(order, (size - 1 - me) % size, size, axis=0)
    return blocks.reshape((size * x.shape[0],) + x.shape[1:])


def frame_starts(clip_lengths, total):
    ends = jnp.cumsum(clip_lengths)
    begins = ends - clip_lengths
    index = jnp.arange(total, dtype=jnp.int32)
    chosen = jnp.where(begins[None, :] <= index[:, None], begins[None, :], 0)
    return jnp.max(chosen, axis=1)


def group_moments(field):
    frames, height, width, chans = field.shape
    group_width = chans // GROUPS
    vals = field.astype(jnp.float32).reshape(frames, height * width, GROUPS, group_width)
    sums = jnp.sum(vals, axis=(1, 3))
    squares = jnp.sum(vals * vals, axis=(1, 3))
    both = lax.psum(jnp.stack([sums, squares]), "band")
    both = lax.psum(lax.optimization_barrier(both), "fsdp")
    sums, squares = both[0], both[1]
    count = height * width * group_width * lax.axis_size("band") * lax.axis_size("fsdp")
    mean = sums / count
    scale = lax.rsqrt(squares / count - mean * mean + EPS)
    return (mean, scale)


def apply_norm(field, mean, scale, gain):
    shape = field.shape
    chans = shape[-1]
    group_width = chans // GROUPS
    vals = field.astype(jnp.float32).reshape(shape[0], -1, GROUPS, group_width)
    normed = (vals - mean[:, None, :, None]) * scale[:, None, :, None]
    return normed.reshape(shape) * gain


def body(video, clip_lengths, norm_gains, spatial_kernel_weight, w_time, w_qkv, w_out):
    frames, height, width, chans = video.shape
    widths = [w.shape[1] for w in (spatial_kernel_weight, w_time, w_qkv, w_out)]
    packed = jnp.concatenate([spatial_kernel_weight, w_time, w_qkv, w_out], axis=1)
    half = packed.shape[1] // 2
    core = lax.axis_index("core")
    mine = lax.dynamic_slice_in_dim(packed, core * half, half, axis=1)
    first_stage = ring_gather(mine, "fsdp")
    second_stage = ring_gather(first_stage, "band")
    other = lax.ppermute(second_stage, "core", [(0, 1), (1, 0)])
    both = jnp.stack([second_stage, other, second_stage])
    gathered = jnp.concatenate(
        [lax.dynamic_index_in_dim(both, core, 0, keepdims=False),
         lax.dynamic_index_in_dim(both, core + 1, 0, keepdims=False)],
        axis=1,
    )
    offsets = [sum(widths[:i]) for i in range(4)]
    space_full, time_full, qkv_full, output_complete = [
        gathered[:, o : o + w] for o, w in zip(offsets, widths)
    ]
    ranks = lax.axis_size(TM)
    total_frames = frames * ranks
    first = lax.axis_index(TM) * frames
    starts = frame_starts(clip_lengths, total_frames)
    local_starts = lax.dynamic_slice_in_dim(starts, first, frames)
    mean_one, scale_one = group_moments(video)
    act = jax.nn.silu(apply_norm(video, mean_one, scale_one, norm_gains[0])).astype(jnp.bfloat16)
    padded = with_halo(act, (("band", 1), ("fsdp", 2)), 1)
    spatial = jnp.zeros((frames, height, width, chans), jnp.float32)
    for tap in range(9):
        shift_y = tap // 3
        shift_x = tap % 3
        spatial = spatial + jnp.einsum(
            "fhwc,cd->fhwd",
            padded[:, shift_y : shift_y + height, shift_x : shift_x + width],
            space_full[:, tap * chans : (tap + 1) * chans],
            preferred_element_type=jnp.float32,
        )
    spatial = spatial.astype(jnp.bfloat16)
    carried = from_behind(spatial[frames - 2 :], TM, 1)
    extended = jnp.concatenate([carried, spatial], axis=0)
    position = first + jnp.arange(frames, dtype=jnp.int32)
    slots = jnp.arange(frames + 2, dtype=jnp.int32)
    temporal = jnp.zeros((frames, height, width, chans), jnp.float32)
    for tap in range(3):
        source = jnp.maximum(position - 2 + tap, local_starts) - first + 2
        select = (source[:, None] == slots[None, :]).astype(jnp.bfloat16)
        picked = jnp.einsum(
            "fe,ehwc->fhwc", select, extended, preferred_element_type=jnp.float32
        ).astype(jnp.bfloat16)
        temporal = temporal + jnp.einsum(
            "fhwc,cd->fhwd",
            picked,
            time_full[:, tap * chans : (tap + 1) * chans],
            preferred_element_type=jnp.float32,
        )
    resid = (video.astype(jnp.float32) + temporal).astype(jnp.bfloat16)
    pixels = height * width
    group_pixels = pixels // ranks
    flat_resid = resid.reshape(frames, ranks, group_pixels, chans).transpose(1, 0, 2, 3)
    received = lax.all_to_all(flat_resid, TM, split_axis=0, concat_axis=0, tiled=True)
    resid_time = received.reshape(total_frames, group_pixels, chans)
    mean_two, scale_two = group_moments(resid)
    moments = jnp.concatenate([mean_two, scale_two], axis=1)
    for axis in TM[::-1]:
        moments = lax.all_gather(moments, axis, axis=0, tiled=True)
    mean_all, scale_all = moments[:, :GROUPS], moments[:, GROUPS:]
    flat_norm = apply_norm(resid_time, mean_all, scale_all, norm_gains[1]).astype(jnp.bfloat16)
    qkv_time = jnp.einsum(
        "fpc,cd->fpd", flat_norm, qkv_full, preferred_element_type=jnp.float32
    ).astype(jnp.bfloat16)
    query = qkv_time[..., :chans]
    keys = qkv_time[..., chans : 2 * chans]
    value_rows = qkv_time[..., 2 * chans :]
    index = jnp.arange(total_frames, dtype=jnp.int32)
    allowed = (index[None, :] <= index[:, None]) & (index[None, :] >= starts[:, None])
    scores = jnp.einsum(
        "fpc,gpc->pfg", query, keys, preferred_element_type=jnp.float32
    ) / math.sqrt(chans)
    scores = jnp.where(allowed[None], scores, -1e30)
    top = jnp.max(scores, axis=-1, keepdims=True)
    expo = jnp.where(allowed[None], jnp.exp(scores - top), 0.0)
    attention_probabilities = (expo / jnp.sum(expo, axis=-1, keepdims=True)).astype(jnp.bfloat16)
    attention_output = jnp.einsum(
        "boh,hba->boa", attention_probabilities, value_rows, preferred_element_type=jnp.float32
    ).astype(jnp.bfloat16)
    projected_output = jnp.einsum(
        "axi,iy->axy", attention_output, output_complete, preferred_element_type=jnp.float32
    )
    mixed = (jnp.swapaxes(resid_time, 0, 1).astype(jnp.float32) + projected_output).astype(
        jnp.bfloat16
    )
    return mixed.reshape(1, 1, mixed.shape[0], total_frames, chans)


def solution(mesh):
    devices = mesh.devices
    split = Mesh(
        devices.reshape((4, devices.shape[0] // 8, 2) + devices.shape[1:]),
        ("zh", "zl", "core", "band", "fsdp"),
    )
    return jax.shard_map(
        body,
        mesh=split,
        in_specs=(
            P(TM, "band", "fsdp", None),
            P(),
            P(),
            P(("band", "fsdp"), None),
            P(("band", "fsdp"), None),
            P(("band", "fsdp"), None),
            P(("band", "fsdp"), None),
        ),
        out_specs=P("band", "fsdp", TM, None, None),
        check_vma=False,
    )
```

```python
import math

import jax
import jax.numpy as jnp
from jax import lax
from jax.sharding import Mesh
from jax.sharding import PartitionSpec as P


GROUPS = 32
TM = ("z", "core")


EPS = 1e-06


def with_halo(x, sides, width):
    for axis, dim in sides:
        size, length = (lax.axis_size(axis), x.shape[dim])
        up = [(i, (i + 1) % size) for i in range(size - 1)]
        down = [(j, i) for i, j in up]
        last = lax.slice_in_dim(x, length - width, length, axis=dim)
        initial = lax.slice_in_dim(x, 0, width, axis=dim)
        before = lax.ppermute(last, axis, up)
        after = lax.ppermute(initial, axis, down)
        x = jnp.concatenate([before, x, after], axis=dim)
    return x


def from_behind(x, axis, by):
    length = lax.axis_size(axis)
    pairs = [(i, i + by) for i in range(length) if 0 <= i + by < length]
    return lax.ppermute(x, axis, pairs)


def ring_gather(x, axis):
    size = lax.axis_size(axis)
    me = lax.axis_index(axis)
    got = [x]
    for shift in range(1, size):
        got.append(lax.ppermute(x, axis, [(i, (i + shift) % size) for i in range(size)]))
    order = jnp.stack(got[::-1] + got[::-1])
    blocks = lax.dynamic_slice_in_dim(order, (size - 1 - me) % size, size, axis=0)
    return blocks.reshape((size * x.shape[0],) + x.shape[1:])


def frame_starts(clip_lengths, total):
    ends = jnp.cumsum(clip_lengths)
    begins = ends - clip_lengths
    index = jnp.arange(total, dtype=jnp.int32)
    chosen = jnp.where(begins[None, :] <= index[:, None], begins[None, :], 0)
    return jnp.max(chosen, axis=1)


def group_moments(field):
    frames, height, width, chans = field.shape
    group_width = chans // GROUPS
    vals = field.astype(jnp.float32).reshape(frames, height * width, GROUPS, group_width)
    sums = jnp.sum(vals, axis=(1, 3))
    squares = jnp.sum(vals * vals, axis=(1, 3))
    both = lax.psum(jnp.stack([sums, squares]), "band")
    both = lax.psum(lax.optimization_barrier(both), "fsdp")
    sums, squares = both[0], both[1]
    count = height * width * group_width * lax.axis_size("band") * lax.axis_size("fsdp")
    mean = sums / count
    scale = lax.rsqrt(squares / count - mean * mean + EPS)
    return (mean, scale)


def apply_norm(field, mean, scale, gain):
    shape = field.shape
    chans = shape[-1]
    group_width = chans // GROUPS
    vals = field.astype(jnp.float32).reshape(shape[0], -1, GROUPS, group_width)
    normed = (vals - mean[:, None, :, None]) * scale[:, None, :, None]
    return normed.reshape(shape) * gain


def body(video, clip_lengths, norm_gains, spatial_kernel_weight, w_time, w_qkv, w_out):
    frames, height, width, chans = video.shape
    widths = [w.shape[1] for w in (spatial_kernel_weight, w_time, w_qkv, w_out)]
    packed = jnp.concatenate([spatial_kernel_weight, w_time, w_qkv, w_out], axis=1)
    half = packed.shape[1] // 2
    core = lax.axis_index("core")
    mine = lax.dynamic_slice_in_dim(packed, core * half, half, axis=1)
    first_stage = ring_gather(mine, "fsdp")
    second_stage = ring_gather(first_stage, "band")
    other = lax.ppermute(second_stage, "core", [(0, 1), (1, 0)])
    both = jnp.stack([second_stage, other, second_stage])
    gathered = jnp.concatenate(
        [lax.dynamic_index_in_dim(both, core, 0, keepdims=False),
         lax.dynamic_index_in_dim(both, core + 1, 0, keepdims=False)],
        axis=1,
    )
    offsets = [sum(widths[:i]) for i in range(4)]
    space_full, time_full, qkv_full, output_complete = [
        gathered[:, o : o + w] for o, w in zip(offsets, widths)
    ]
    ranks = lax.axis_size(TM)
    total_frames = frames * ranks
    first = lax.axis_index(TM) * frames
    starts = frame_starts(clip_lengths, total_frames)
    local_starts = lax.dynamic_slice_in_dim(starts, first, frames)
    mean_one, scale_one = group_moments(video)
    act = jax.nn.silu(apply_norm(video, mean_one, scale_one, norm_gains[0])).astype(jnp.bfloat16)
    padded = with_halo(act, (("band", 1), ("fsdp", 2)), 1)
    spatial = jnp.zeros((frames, height, width, chans), jnp.float32)
    for tap in range(9):
        shift_y = tap // 3
        shift_x = tap % 3
        spatial = spatial + jnp.einsum(
            "fhwc,cd->fhwd",
            padded[:, shift_y : shift_y + height, shift_x : shift_x + width],
            space_full[:, tap * chans : (tap + 1) * chans],
            preferred_element_type=jnp.float32,
        )
    spatial = spatial.astype(jnp.bfloat16)
    carried = from_behind(spatial[frames - 2 :], TM, 1)
    extended = jnp.concatenate([carried, spatial], axis=0)
    position = first + jnp.arange(frames, dtype=jnp.int32)
    slots = jnp.arange(frames + 2, dtype=jnp.int32)
    picks = []
    for tap in range(3):
        source = jnp.maximum(position - 2 + tap, local_starts) - first + 2
        select = (source[:, None] == slots[None, :]).astype(jnp.bfloat16)
        picks.append(
            jnp.einsum(
                "fe,ehwc->fhwc", select, extended, preferred_element_type=jnp.float32
            ).astype(jnp.bfloat16)
        )
    stacked_taps = jnp.concatenate(
        [time_full[:, tap * chans : (tap + 1) * chans] for tap in range(3)], axis=0
    )
    temporal = jnp.einsum(
        "fhwc,cd->fhwd",
        jnp.concatenate(picks, axis=-1),
        stacked_taps,
        preferred_element_type=jnp.float32,
    )
    resid = (video.astype(jnp.float32) + temporal).astype(jnp.bfloat16)
    pixels = height * width
    group_pixels = pixels // ranks
    flat_resid = resid.reshape(frames, ranks, group_pixels, chans).transpose(1, 0, 2, 3)
    received = lax.all_to_all(flat_resid, TM, split_axis=0, concat_axis=0, tiled=True)
    resid_time = received.reshape(total_frames, group_pixels, chans)
    mean_two, scale_two = group_moments(resid)
    moments = jnp.concatenate([mean_two, scale_two], axis=1)
    for axis in TM[::-1]:
        moments = lax.all_gather(moments, axis, axis=0, tiled=True)
    mean_all, scale_all = moments[:, :GROUPS], moments[:, GROUPS:]
    flat_norm = apply_norm(resid_time, mean_all, scale_all, norm_gains[1]).astype(jnp.bfloat16)
    qkv_time = jnp.einsum(
        "fpc,cd->fpd", flat_norm, qkv_full, preferred_element_type=jnp.float32
    ).astype(jnp.bfloat16)
    query = qkv_time[..., :chans]
    keys = qkv_time[..., chans : 2 * chans]
    value_rows = qkv_time[..., 2 * chans :]
    index = jnp.arange(total_frames, dtype=jnp.int32)
    allowed = (index[None, :] <= index[:, None]) & (index[None, :] >= starts[:, None])
    scores = jnp.einsum(
        "fpc,gpc->pfg", query, keys, preferred_element_type=jnp.float32
    ) / math.sqrt(chans)
    scores = jnp.where(allowed[None], scores, -1e30)
    top = jnp.max(scores, axis=-1, keepdims=True)
    expo = jnp.where(allowed[None], jnp.exp(scores - top), 0.0)
    attention_probabilities = (expo / jnp.sum(expo, axis=-1, keepdims=True)).astype(jnp.bfloat16)
    attention_output = jnp.einsum(
        "boh,hba->boa", attention_probabilities, value_rows, preferred_element_type=jnp.float32
    ).astype(jnp.bfloat16)
    projected_output = jnp.einsum(
        "axi,iy->axy", attention_output, output_complete, preferred_element_type=jnp.float32
    )
    mixed = (jnp.swapaxes(resid_time, 0, 1).astype(jnp.float32) + projected_output).astype(
        jnp.bfloat16
    )
    return mixed.reshape(1, 1, mixed.shape[0], total_frames, chans)


def solution(mesh):
    devices = mesh.devices
    split = Mesh(
        devices.reshape((devices.shape[0] // 2, 2) + devices.shape[1:]),
        ("z", "core", "band", "fsdp"),
    )
    return jax.shard_map(
        body,
        mesh=split,
        in_specs=(
            P(TM, "band", "fsdp", None),
            P(),
            P(),
            P(("band", "fsdp"), None),
            P(("band", "fsdp"), None),
            P(("band", "fsdp"), None),
            P(("band", "fsdp"), None),
        ),
        out_specs=P("band", "fsdp", TM, None, None),
        check_vma=False,
    )
```

```python
import math

import jax
import jax.numpy as jnp
from jax import lax
from jax.sharding import Mesh
from jax.sharding import PartitionSpec as P


GROUPS = 32
TM = ("z", "core")


EPS = 1e-06


def with_halo(x, sides, width):
    for axis, dim in sides:
        size, length = (lax.axis_size(axis), x.shape[dim])
        up = [(i, (i + 1) % size) for i in range(size - 1)]
        down = [(j, i) for i, j in up]
        last = lax.slice_in_dim(x, length - width, length, axis=dim)
        initial = lax.slice_in_dim(x, 0, width, axis=dim)
        before = lax.ppermute(last, axis, up)
        after = lax.ppermute(initial, axis, down)
        x = jnp.concatenate([before, x, after], axis=dim)
    return x


def from_behind(x, axis, by):
    length = lax.axis_size(axis)
    pairs = [(i, i + by) for i in range(length) if 0 <= i + by < length]
    return lax.ppermute(x, axis, pairs)


def ring_gather(x, axis):
    size = lax.axis_size(axis)
    me = lax.axis_index(axis)
    got = [x]
    for shift in range(1, size):
        got.append(lax.ppermute(x, axis, [(i, (i + shift) % size) for i in range(size)]))
    order = jnp.stack(got[::-1] + got[::-1])
    blocks = lax.dynamic_slice_in_dim(order, (size - 1 - me) % size, size, axis=0)
    return blocks.reshape((size * x.shape[0],) + x.shape[1:])


def frame_starts(clip_lengths, total):
    ends = jnp.cumsum(clip_lengths)
    begins = ends - clip_lengths
    index = jnp.arange(total, dtype=jnp.int32)
    chosen = jnp.where(begins[None, :] <= index[:, None], begins[None, :], 0)
    return jnp.max(chosen, axis=1)


def group_moments(field):
    frames, height, width, chans = field.shape
    group_width = chans // GROUPS
    vals = field.astype(jnp.float32).reshape(frames, height * width, GROUPS, group_width)
    sums = jnp.sum(vals, axis=(1, 3))
    squares = jnp.sum(vals * vals, axis=(1, 3))
    both = lax.psum(jnp.stack([sums, squares]), "band")
    both = lax.psum(lax.optimization_barrier(both), "fsdp")
    sums, squares = both[0], both[1]
    count = height * width * group_width * lax.axis_size("band") * lax.axis_size("fsdp")
    mean = sums / count
    scale = lax.rsqrt(squares / count - mean * mean + EPS)
    return (mean, scale)


def apply_norm(field, mean, scale, gain):
    shape = field.shape
    chans = shape[-1]
    group_width = chans // GROUPS
    vals = field.astype(jnp.float32).reshape(shape[0], -1, GROUPS, group_width)
    normed = (vals - mean[:, None, :, None]) * scale[:, None, :, None]
    return normed.reshape(shape) * gain


def body(video, clip_lengths, norm_gains, spatial_kernel_weight, w_time, w_qkv, w_out):
    frames, height, width, chans = video.shape
    widths = [w.shape[1] for w in (spatial_kernel_weight, w_time, w_qkv, w_out)]
    packed = jnp.concatenate([spatial_kernel_weight, w_time, w_qkv, w_out], axis=1)
    half = packed.shape[1] // 2
    core = lax.axis_index("core")
    mine = lax.dynamic_slice_in_dim(packed, core * half, half, axis=1)
    first_stage = ring_gather(mine, "fsdp")
    second_stage = ring_gather(first_stage, "band")
    other = lax.ppermute(second_stage, "core", [(0, 1), (1, 0)])
    both = jnp.stack([second_stage, other, second_stage])
    gathered = jnp.concatenate(
        [lax.dynamic_index_in_dim(both, core, 0, keepdims=False),
         lax.dynamic_index_in_dim(both, core + 1, 0, keepdims=False)],
        axis=1,
    )
    offsets = [sum(widths[:i]) for i in range(4)]
    space_full, time_full, qkv_full, output_complete = [
        gathered[:, o : o + w] for o, w in zip(offsets, widths)
    ]
    ranks = lax.axis_size(TM)
    total_frames = frames * ranks
    first = lax.axis_index(TM) * frames
    starts = frame_starts(clip_lengths, total_frames)
    local_starts = lax.dynamic_slice_in_dim(starts, first, frames)
    mean_one, scale_one = group_moments(video)
    act = jax.nn.silu(apply_norm(video, mean_one, scale_one, norm_gains[0])).astype(jnp.bfloat16)
    padded = with_halo(act, (("band", 1), ("fsdp", 2)), 1)
    spatial = jnp.zeros((frames, height, width, chans), jnp.float32)
    for tap in range(9):
        shift_y = tap // 3
        shift_x = tap % 3
        spatial = spatial + jnp.einsum(
            "fhwc,cd->fhwd",
            padded[:, shift_y : shift_y + height, shift_x : shift_x + width],
            space_full[:, tap * chans : (tap + 1) * chans],
            preferred_element_type=jnp.float32,
        )
    spatial = spatial.astype(jnp.bfloat16)
    carried = from_behind(spatial[frames - 2 :], TM, 1)
    extended = jnp.concatenate([carried, spatial], axis=0)
    position = first + jnp.arange(frames, dtype=jnp.int32)
    temporal = jnp.zeros((frames, height, width, chans), jnp.float32)
    for tap in range(3):
        source = jnp.maximum(position - 2 + tap, local_starts) - first + 2
        picked = jnp.take(extended, source, axis=0, mode="clip")
        temporal = temporal + jnp.einsum(
            "fhwc,cd->fhwd",
            picked,
            time_full[:, tap * chans : (tap + 1) * chans],
            preferred_element_type=jnp.float32,
        )
    resid = (video.astype(jnp.float32) + temporal).astype(jnp.bfloat16)
    pixels = height * width
    group_pixels = pixels // ranks
    flat_resid = resid.reshape(frames, ranks, group_pixels, chans).transpose(1, 0, 2, 3)
    received = lax.all_to_all(flat_resid, TM, split_axis=0, concat_axis=0, tiled=True)
    resid_time = received.reshape(total_frames, group_pixels, chans)
    mean_two, scale_two = group_moments(resid)
    moments = jnp.concatenate([mean_two, scale_two], axis=1)
    for axis in TM[::-1]:
        moments = lax.all_gather(moments, axis, axis=0, tiled=True)
    mean_all, scale_all = moments[:, :GROUPS], moments[:, GROUPS:]
    flat_norm = apply_norm(resid_time, mean_all, scale_all, norm_gains[1]).astype(jnp.bfloat16)
    qkv_time = jnp.einsum(
        "fpc,cd->fpd", flat_norm, qkv_full, preferred_element_type=jnp.float32
    ).astype(jnp.bfloat16)
    query = qkv_time[..., :chans]
    keys = qkv_time[..., chans : 2 * chans]
    value_rows = qkv_time[..., 2 * chans :]
    index = jnp.arange(total_frames, dtype=jnp.int32)
    allowed = (index[None, :] <= index[:, None]) & (index[None, :] >= starts[:, None])
    scores = jnp.einsum(
        "fpc,gpc->pfg", query, keys, preferred_element_type=jnp.float32
    ) / math.sqrt(chans)
    scores = jnp.where(allowed[None], scores, -1e30)
    top = jnp.max(scores, axis=-1, keepdims=True)
    expo = jnp.where(allowed[None], jnp.exp(scores - top), 0.0)
    attention_probabilities = (expo / jnp.sum(expo, axis=-1, keepdims=True)).astype(jnp.bfloat16)
    attention_output = jnp.einsum(
        "boh,hba->boa", attention_probabilities, value_rows, preferred_element_type=jnp.float32
    ).astype(jnp.bfloat16)
    projected_output = jnp.einsum(
        "axi,iy->axy", attention_output, output_complete, preferred_element_type=jnp.float32
    )
    mixed = (jnp.swapaxes(resid_time, 0, 1).astype(jnp.float32) + projected_output).astype(
        jnp.bfloat16
    )
    return mixed.reshape(1, 1, mixed.shape[0], total_frames, chans)


def solution(mesh):
    devices = mesh.devices
    split = Mesh(
        devices.reshape((devices.shape[0] // 2, 2) + devices.shape[1:]),
        ("z", "core", "band", "fsdp"),
    )
    return jax.shard_map(
        body,
        mesh=split,
        in_specs=(
            P(TM, "band", "fsdp", None),
            P(),
            P(),
            P(("band", "fsdp"), None),
            P(("band", "fsdp"), None),
            P(("band", "fsdp"), None),
            P(("band", "fsdp"), None),
        ),
        out_specs=P("band", "fsdp", TM, None, None),
        check_vma=False,
    )
```

```python
import math

import jax
import jax.numpy as jnp
from jax import lax
from jax.sharding import Mesh
from jax.sharding import PartitionSpec as P


GROUPS = 32
TM = ("z", "core")


EPS = 1e-06


def with_halo(x, sides, width):
    for axis, dim in sides:
        size, length = (lax.axis_size(axis), x.shape[dim])
        up = [(i, (i + 1) % size) for i in range(size - 1)]
        down = [(j, i) for i, j in up]
        last = lax.slice_in_dim(x, length - width, length, axis=dim)
        initial = lax.slice_in_dim(x, 0, width, axis=dim)
        before = lax.ppermute(last, axis, up)
        after = lax.ppermute(initial, axis, down)
        x = jnp.concatenate([before, x, after], axis=dim)
    return x


def from_behind(x, axis, by):
    length = lax.axis_size(axis)
    pairs = [(i, i + by) for i in range(length) if 0 <= i + by < length]
    return lax.ppermute(x, axis, pairs)


def ring_gather(x, axis):
    size = lax.axis_size(axis)
    me = lax.axis_index(axis)
    got = [x]
    for shift in range(1, size):
        got.append(lax.ppermute(x, axis, [(i, (i + shift) % size) for i in range(size)]))
    order = jnp.stack(got[::-1] + got[::-1])
    blocks = lax.dynamic_slice_in_dim(order, (size - 1 - me) % size, size, axis=0)
    return blocks.reshape((size * x.shape[0],) + x.shape[1:])


def frame_starts(clip_lengths, total):
    ends = jnp.cumsum(clip_lengths)
    begins = ends - clip_lengths
    index = jnp.arange(total, dtype=jnp.int32)
    chosen = jnp.where(begins[None, :] <= index[:, None], begins[None, :], 0)
    return jnp.max(chosen, axis=1)


def group_moments(field, order=("band", "fsdp")):
    frames, height, width, chans = field.shape
    group_width = chans // GROUPS
    vals = field.astype(jnp.float32).reshape(frames, height * width, GROUPS, group_width)
    sums = jnp.sum(vals, axis=(1, 3))
    squares = jnp.sum(vals * vals, axis=(1, 3))
    both = lax.psum(jnp.stack([sums, squares]), order[0])
    both = lax.psum(lax.optimization_barrier(both), order[1])
    sums, squares = both[0], both[1]
    count = height * width * group_width * lax.axis_size("band") * lax.axis_size("fsdp")
    mean = sums / count
    scale = lax.rsqrt(squares / count - mean * mean + EPS)
    return (mean, scale)


def apply_norm(field, mean, scale, gain):
    shape = field.shape
    chans = shape[-1]
    group_width = chans // GROUPS
    vals = field.astype(jnp.float32).reshape(shape[0], -1, GROUPS, group_width)
    normed = (vals - mean[:, None, :, None]) * scale[:, None, :, None]
    return normed.reshape(shape) * gain


def body(video, clip_lengths, norm_gains, spatial_kernel_weight, w_time, w_qkv, w_out):
    frames, height, width, chans = video.shape
    widths = [w.shape[1] for w in (spatial_kernel_weight, w_time, w_qkv, w_out)]
    packed = jnp.concatenate([spatial_kernel_weight, w_time, w_qkv, w_out], axis=1)
    half = packed.shape[1] // 2
    core = lax.axis_index("core")
    mine = lax.dynamic_slice_in_dim(packed, core * half, half, axis=1)
    first_stage = ring_gather(mine, "fsdp")
    second_stage = ring_gather(first_stage, "band")
    other = lax.ppermute(second_stage, "core", [(0, 1), (1, 0)])
    both = jnp.stack([second_stage, other, second_stage])
    gathered = jnp.concatenate(
        [lax.dynamic_index_in_dim(both, core, 0, keepdims=False),
         lax.dynamic_index_in_dim(both, core + 1, 0, keepdims=False)],
        axis=1,
    )
    offsets = [sum(widths[:i]) for i in range(4)]
    space_full, time_full, qkv_full, output_complete = [
        gathered[:, o : o + w] for o, w in zip(offsets, widths)
    ]
    ranks = lax.axis_size(TM)
    total_frames = frames * ranks
    first = lax.axis_index(TM) * frames
    starts = frame_starts(clip_lengths, total_frames)
    local_starts = lax.dynamic_slice_in_dim(starts, first, frames)
    mean_one, scale_one = group_moments(video, ("fsdp", "band"))
    act = jax.nn.silu(apply_norm(video, mean_one, scale_one, norm_gains[0])).astype(jnp.bfloat16)
    padded = with_halo(act, (("band", 1), ("fsdp", 2)), 1)
    spatial = jnp.zeros((frames, height, width, chans), jnp.float32)
    for tap in range(9):
        shift_y = tap // 3
        shift_x = tap % 3
        spatial = spatial + jnp.einsum(
            "fhwc,cd->fhwd",
            padded[:, shift_y : shift_y + height, shift_x : shift_x + width],
            space_full[:, tap * chans : (tap + 1) * chans],
            preferred_element_type=jnp.float32,
        )
    spatial = spatial.astype(jnp.bfloat16)
    carried = from_behind(spatial[frames - 2 :], TM, 1)
    extended = jnp.concatenate([carried, spatial], axis=0)
    position = first + jnp.arange(frames, dtype=jnp.int32)
    slots = jnp.arange(frames + 2, dtype=jnp.int32)
    temporal = jnp.zeros((frames, height, width, chans), jnp.float32)
    for tap in range(3):
        source = jnp.maximum(position - 2 + tap, local_starts) - first + 2
        select = (source[:, None] == slots[None, :]).astype(jnp.bfloat16)
        picked = jnp.einsum(
            "fe,ehwc->fhwc", select, extended, preferred_element_type=jnp.float32
        ).astype(jnp.bfloat16)
        temporal = temporal + jnp.einsum(
            "fhwc,cd->fhwd",
            picked,
            time_full[:, tap * chans : (tap + 1) * chans],
            preferred_element_type=jnp.float32,
        )
    resid = (video.astype(jnp.float32) + temporal).astype(jnp.bfloat16)
    pixels = height * width
    group_pixels = pixels // ranks
    flat_resid = resid.reshape(frames, ranks, group_pixels, chans).transpose(1, 0, 2, 3)
    received = lax.all_to_all(flat_resid, TM, split_axis=0, concat_axis=0, tiled=True)
    resid_time = received.reshape(total_frames, group_pixels, chans)
    mean_two, scale_two = group_moments(resid)
    moments = jnp.concatenate([mean_two, scale_two], axis=1)
    for axis in TM[::-1]:
        moments = lax.all_gather(moments, axis, axis=0, tiled=True)
    mean_all, scale_all = moments[:, :GROUPS], moments[:, GROUPS:]
    flat_norm = apply_norm(resid_time, mean_all, scale_all, norm_gains[1]).astype(jnp.bfloat16)
    qkv_time = jnp.einsum(
        "fpc,cd->fpd", flat_norm, qkv_full, preferred_element_type=jnp.float32
    ).astype(jnp.bfloat16)
    query = qkv_time[..., :chans]
    keys = qkv_time[..., chans : 2 * chans]
    value_rows = qkv_time[..., 2 * chans :]
    index = jnp.arange(total_frames, dtype=jnp.int32)
    allowed = (index[None, :] <= index[:, None]) & (index[None, :] >= starts[:, None])
    scores = jnp.einsum(
        "fpc,gpc->pfg", query, keys, preferred_element_type=jnp.float32
    ) / math.sqrt(chans)
    scores = jnp.where(allowed[None], scores, -1e30)
    top = jnp.max(scores, axis=-1, keepdims=True)
    expo = jnp.where(allowed[None], jnp.exp(scores - top), 0.0)
    attention_probabilities = (expo / jnp.sum(expo, axis=-1, keepdims=True)).astype(jnp.bfloat16)
    attention_output = jnp.einsum(
        "boh,hba->boa", attention_probabilities, value_rows, preferred_element_type=jnp.float32
    ).astype(jnp.bfloat16)
    projected_output = jnp.einsum(
        "axi,iy->axy", attention_output, output_complete, preferred_element_type=jnp.float32
    )
    mixed = (jnp.swapaxes(resid_time, 0, 1).astype(jnp.float32) + projected_output).astype(
        jnp.bfloat16
    )
    return mixed.reshape(1, 1, mixed.shape[0], total_frames, chans)


def solution(mesh):
    devices = mesh.devices
    split = Mesh(
        devices.reshape((devices.shape[0] // 2, 2) + devices.shape[1:]),
        ("z", "core", "band", "fsdp"),
    )
    return jax.shard_map(
        body,
        mesh=split,
        in_specs=(
            P(TM, "band", "fsdp", None),
            P(),
            P(),
            P(("band", "fsdp"), None),
            P(("band", "fsdp"), None),
            P(("band", "fsdp"), None),
            P(("band", "fsdp"), None),
        ),
        out_specs=P("band", "fsdp", TM, None, None),
        check_vma=False,
    )
```
